32 devices in a mesh: gx: 4 (over y, x), gy: 8 (over z, core).
Axes of the slice: x: 2, y: 2, z: 4, core: 2. Of those that a mesh axis runs over, the one named last changes fastest.
Arguments:
- start_field: float32 [64, 64, 512], P('gx', 'gy'), may hold values from -6 to 6
- right_side: float32 [64, 64, 512], P('gx', 'gy'), may hold values from -12 to 12
- accumulation: float32 [64, 64, 512], P('gx', 'gy'), may hold values from 0.05 to 1
- trans_x: float32 [64, 64, 512], P('gx', 'gy'), may hold values from 0.1 to 10
- trans_y: float32 [64, 64, 512], P('gx', 'gy'), may hold values from 0.1 to 10
- trans_z: float32 [64, 64, 512], P('gx', 'gy'), may hold values from 0.1 to 10
Outputs:
- ortho_basis: float32 [5, 64, 64, 512], P(None, 'gx', 'gy')
- upper_factor: float32 [5, 5], replicated
- residual_scale: float32 [], replicated
The draws below stay inside these ranges and needn't reach their ends.
All inputs are finite; a program needn't handle non-finite values.
Results may differ from the reference program's by a relative error of at most 0.0003.
Values sent between devices are 32-bit elements; how exact they have to be, the bound alone decides.
No kernel may reach another device: no remote copies, remote signals or barrier semaphores. Data moves between devices by JAX's collectives and lax.ppermute only.
A program may use at most 64 MiB of HBM per device.

```python
import math
import jax
import jax.numpy as jnp
from jax import lax

NZ = 512
STEPS = 4
NX = 64
NY = 64


def draw_right_side(key, part):
    ix = jnp.arange(NX, dtype=jnp.float32)[:, None, None] / NX
    iy = jnp.arange(NY, dtype=jnp.float32)[None, :, None] / NY
    ramp = 1.0 + ix + iy
    noise = jnp.clip(jax.random.normal(key, (NX, NY, NZ), jnp.float32), -4.0, 4.0)
    return (noise * ramp).astype(jnp.float32)


def shard_levels(key, extent, split, low, top_value):
    gain = 1.0
    for dim, shards_of in split:
        steps = jax.random.uniform(jax.random.fold_in(jax.random.fold_in(key, 6), dim), (shards_of,), jnp.float32, low / len(split), top_value / len(split))
        gain = gain * jnp.repeat(jnp.exp(steps), extent[dim] // shards_of).reshape((-1,) + (1,) * (len(extent) - 1 - dim))
    return gain


def gaussian(own_key, dims, deviation, limit, shards=(), kind=jnp.bfloat16):
    array = deviation * jax.random.normal(own_key, dims, jnp.float32)
    if shards:
        array = array * shard_levels(own_key, dims, shards, -0.22, 0.18)
    return jnp.clip(array, -limit, limit).astype(kind)


def setup_inputs(seed: int = 0) -> dict:
    streams_of = jax.random.split(jax.random.key(seed), 7)
    return {
        "start_field": gaussian(streams_of[0], (NX, NY, NZ), 1.0, 6.0, ((0, 4), (1, 8)), jnp.float32),
        "right_side": draw_right_side(jax.random.fold_in(streams_of[6], 71), 0),
        "accumulation": jnp.clip(jnp.exp(math.log(1.0) - 2.9957323 * jax.random.uniform(streams_of[2], (NX, NY, NZ), jnp.float32) ** shard_levels(streams_of[2], (NX, NY, NZ), ((0, 4), (1, 8)), -0.2, 0.2)), 0.05, 1.0),
        "trans_x": jnp.clip(jnp.exp(math.log(10.0) - 4.6051702 * jax.random.uniform(streams_of[3], (NX, NY, NZ), jnp.float32) ** shard_levels(streams_of[3], (NX, NY, NZ), ((0, 4), (1, 8)), -0.2, 0.2)), 0.1, 10.0),
        "trans_y": jnp.clip(jnp.exp(math.log(10.0) - 4.6051702 * jax.random.uniform(streams_of[4], (NX, NY, NZ), jnp.float32) ** shard_levels(streams_of[4], (NX, NY, NZ), ((0, 4), (1, 8)), -0.2, 0.2)), 0.1, 10.0),
        "trans_z": jnp.clip(jnp.exp(math.log(10.0) - 4.6051702 * jax.random.uniform(streams_of[5], (NX, NY, NZ), jnp.float32) ** shard_levels(streams_of[5], (NX, NY, NZ), ((0, 4), (1, 8)), -0.2, 0.2)), 0.1, 10.0),
    }


EPS = 1e-06

def neighbours(field, coef):
    acc_c, t_x, t_y, t_z = coef
    lx = field.shape[0] - 2
    ly = field.shape[1] - 2
    ox = (t_x.shape[0] - lx) // 2
    oy = (t_x.shape[1] - ly) // 2

    def piece(a, dx, dy):
        return a[ox + dx:ox + dx + lx, oy + dy:oy + dy + ly]
    centre = field[1:-1, 1:-1]
    zero_plane = jnp.zeros_like(centre[..., :1])
    tz_low = piece(t_z, 0, 0)
    tz_high = jnp.concatenate([tz_low[..., 1:], zero_plane], axis=-1)
    z_low = jnp.concatenate([zero_plane, centre[..., :-1]], axis=-1)
    z_high = jnp.concatenate([centre[..., 1:], zero_plane], axis=-1)
    tx_low = piece(t_x, 0, 0)
    tx_high = piece(t_x, 1, 0)
    ty_low = piece(t_y, 0, 0)
    ty_high = piece(t_y, 0, 1)
    total = tx_low * field[:-2, 1:-1] + tx_high * field[2:, 1:-1]
    total = total + ty_low * field[1:-1, :-2] + ty_high * field[1:-1, 2:]
    total = total + tz_low * z_low + tz_high * z_high
    diagonal = piece(acc_c, 0, 0) + tx_low + tx_high + ty_low + ty_high + tz_low + tz_high
    return (total, diagonal)

def upper_inverse(upper):
    size = upper.shape[0]
    columns = []
    for col in range(size):
        values = [None] * size
        for row in reversed(range(size)):
            value = jnp.float32(1.0 if row == col else 0.0)
            for inner in range(row + 1, size):
                value = value - upper[row, inner] * values[inner]
            values[row] = value / upper[row, row]
        columns.append(jnp.stack(values))
    return jnp.stack(columns, axis=1)

def widen(a):
    return jnp.pad(a, ((1, 1), (1, 1), (0, 0)))

def reference(start_field, right_side, accumulation, trans_x, trans_y, trans_z):
    coef = (widen(accumulation), widen(trans_x), widen(trans_y), widen(trans_z))
    total, diagonal = neighbours(widen(start_field), coef)
    residual0 = right_side - (diagonal * start_field - total)
    cells = residual0.size
    scale = jnp.sqrt(jnp.sum(residual0 * residual0) / cells + EPS)
    vector = residual0 / scale
    basis = [vector]
    for step in range(STEPS):
        total, diagonal = neighbours(widen(vector), coef)
        vector = 2.0 * total / diagonal
        basis.append(vector)
    stacked = jnp.stack(basis)
    gram = jnp.einsum('axyz,bxyz->ab', stacked, stacked, precision=lax.Precision.HIGHEST) / cells
    upper = jnp.linalg.cholesky(gram).T
    inverse = upper_inverse(upper)
    ortho = jnp.einsum('jk,jxyz->kxyz', inverse, stacked, precision=lax.Precision.HIGHEST)
    return (ortho, upper, scale)
```

```python
import jax
import jax.numpy as jnp
from jax import lax
from jax.sharding import PartitionSpec as P

STEPS = 4


EPS = 1e-06


def shift_pairs(axis, by):
    peers = lax.axis_size(axis)
    return [(i, i + by) for i in range(peers) if 0 <= i + by < peers]


def exchange(to_low_x, to_high_x, to_low_y, to_high_y):
    from_high_x = lax.ppermute(to_low_x, "gx", shift_pairs("gx", -1))
    from_low_x = lax.ppermute(to_high_x, "gx", shift_pairs("gx", 1))
    from_high_y = lax.ppermute(to_low_y, "gy", shift_pairs("gy", -1))
    from_low_y = lax.ppermute(to_high_y, "gy", shift_pairs("gy", 1))
    return from_low_x, from_high_x, from_low_y, from_high_y


def neighbour_sum(u, halo, coef):
    lo_x, hi_x, lo_y, hi_y = halo
    tx_lo, tx_hi, ty_lo, ty_hi, tz_lo, tz_hi = coef
    zero_plane = jnp.zeros_like(u[..., :1])
    u_xm = jnp.concatenate([lo_x, u[:-1]], axis=0)
    u_xp = jnp.concatenate([u[1:], hi_x], axis=0)
    u_ym = jnp.concatenate([lo_y, u[:, :-1]], axis=1)
    u_yp = jnp.concatenate([u[:, 1:], hi_y], axis=1)
    u_zm = jnp.concatenate([zero_plane, u[..., :-1]], axis=-1)
    u_zp = jnp.concatenate([u[..., 1:], zero_plane], axis=-1)
    total = tx_lo * u_xm + tx_hi * u_xp
    total = total + ty_lo * u_ym + ty_hi * u_yp
    total = total + tz_lo * u_zm + tz_hi * u_zp
    return total


def field_halo(u):
    return exchange(u[:1], u[-1:], u[:, :1], u[:, -1:])


def all_sum(x):
    for axis in ("gy", "gx"):
        n = lax.axis_size(axis)
        if n & (n - 1):
            x = lax.psum(x, axis)
            continue
        step = 1
        while step < n:
            x = x + lax.ppermute(x, axis, [(i, i ^ step) for i in range(n)])
            step *= 2
    return x


def cholesky_upper(gram):
    size = gram.shape[0]
    rows = []
    for row in range(size):
        cur = gram[row]
        for prev in range(row):
            cur = cur - rows[prev][row] * rows[prev]
        pivot = jnp.sqrt(cur[row])
        mask = jnp.arange(size) >= row
        rows.append(jnp.where(mask, cur / pivot, 0.0))
    return jnp.stack(rows)


def upper_inverse(upper):
    size = upper.shape[0]
    eye = jnp.eye(size, dtype=upper.dtype)
    rows = [None] * size
    for row in reversed(range(size)):
        value = eye[row]
        for inner in range(row + 1, size):
            value = value - upper[row, inner] * rows[inner]
        rows[row] = value / upper[row, row]
    return jnp.stack(rows)


def local(start_field, right_side, accumulation, trans_x, trans_y, trans_z):
    size_x, size_y, size_z = start_field.shape
    cells = size_x * size_y * size_z * lax.axis_size("gx") * lax.axis_size("gy")

    lo_x, hi_both_x, lo_y, hi_both_y = exchange(
        jnp.concatenate([start_field[:1], trans_x[:1]], axis=0),
        start_field[-1:],
        jnp.concatenate([start_field[:, :1], trans_y[:, :1]], axis=1),
        start_field[:, -1:],
    )
    hi_x, plane_x = hi_both_x[:1], hi_both_x[1:]
    hi_y, plane_y = hi_both_y[:, :1], hi_both_y[:, 1:]

    zero_plane = jnp.zeros_like(trans_z[..., :1])
    tx_lo = trans_x
    tx_hi = jnp.concatenate([trans_x[1:], plane_x], axis=0)
    ty_lo = trans_y
    ty_hi = jnp.concatenate([trans_y[:, 1:], plane_y], axis=1)
    tz_lo = trans_z
    tz_hi = jnp.concatenate([trans_z[..., 1:], zero_plane], axis=-1)
    coef = (tx_lo, tx_hi, ty_lo, ty_hi, tz_lo, tz_hi)
    diagonal = accumulation + tx_lo + tx_hi + ty_lo + ty_hi + tz_lo + tz_hi

    total = neighbour_sum(start_field, (lo_x, hi_x, lo_y, hi_y), coef)
    residual0 = right_side - (diagonal * start_field - total)

    vector = residual0
    basis = [vector]
    for step in range(STEPS):
        total = neighbour_sum(vector, field_halo(vector), coef)
        vector = 2.0 * total / diagonal
        basis.append(vector)
    block = jnp.stack(basis)
    local_gram = jnp.einsum("axyz,bxyz->ab", block, block, precision=lax.Precision.HIGHEST)
    squares = jnp.sum(residual0 * residual0)
    stats = jnp.concatenate([squares[None], local_gram.reshape(-1)])
    stats = all_sum(stats)
    scale = jnp.sqrt(stats[0] / cells + EPS)
    gram = stats[1:].reshape(local_gram.shape) / cells / (scale * scale)
    upper = cholesky_upper(gram)
    inverse = upper_inverse(upper) / scale
    ortho = jnp.einsum("jk,jxyz->kxyz", inverse, block, precision=lax.Precision.HIGHEST)
    return (ortho, upper, scale)


def solution(mesh):
    in_specs = (
        P("gx", "gy", None),
        P("gx", "gy", None),
        P("gx", "gy", None),
        P("gx", "gy", None),
        P("gx", "gy", None),
        P("gx", "gy", None),
    )
    out_specs = (P(None, "gx", "gy", None), P(), P())
    return jax.shard_map(local, mesh=mesh, in_specs=in_specs, out_specs=out_specs, check_vma=False)
```

```python
import jax
import jax.numpy as jnp
from jax import lax
from jax.sharding import PartitionSpec as P
from jax.experimental import pallas as pl
from jax.experimental.pallas import tpu as pltpu

STEPS = 4


EPS = 1e-06


def shift_pairs(axis, by):
    peers = lax.axis_size(axis)
    return [(i, i + by) for i in range(peers) if 0 <= i + by < peers]


def exchange(to_low_x, to_high_x, to_low_y, to_high_y):
    from_high_x = lax.ppermute(to_low_x, "gx", shift_pairs("gx", -1))
    from_low_x = lax.ppermute(to_high_x, "gx", shift_pairs("gx", 1))
    from_high_y = lax.ppermute(to_low_y, "gy", shift_pairs("gy", -1))
    from_low_y = lax.ppermute(to_high_y, "gy", shift_pairs("gy", 1))
    return from_low_x, from_high_x, from_low_y, from_high_y


def neighbour_sum(u, halo, coef):
    lo_x, hi_x, lo_y, hi_y = halo
    tx_lo, tx_hi, ty_lo, ty_hi, tz_lo, tz_hi = coef
    zero_plane = jnp.zeros_like(u[..., :1])
    u_xm = jnp.concatenate([lo_x, u[:-1]], axis=0)
    u_xp = jnp.concatenate([u[1:], hi_x], axis=0)
    u_ym = jnp.concatenate([lo_y, u[:, :-1]], axis=1)
    u_yp = jnp.concatenate([u[:, 1:], hi_y], axis=1)
    u_zm = jnp.concatenate([zero_plane, u[..., :-1]], axis=-1)
    u_zp = jnp.concatenate([u[..., 1:], zero_plane], axis=-1)
    total = tx_lo * u_xm + tx_hi * u_xp
    total = total + ty_lo * u_ym + ty_hi * u_yp
    total = total + tz_lo * u_zm + tz_hi * u_zp
    return total


def field_halo(u):
    return exchange(u[:1], u[-1:], u[:, :1], u[:, -1:])


def all_sum(x):
    for axis in ("gy", "gx"):
        n = lax.axis_size(axis)
        if n & (n - 1):
            x = lax.psum(x, axis)
            continue
        step = 1
        while step < n:
            x = x + lax.ppermute(x, axis, [(i, i ^ step) for i in range(n)])
            step *= 2
    return x


def finish_kernel(cells, size, stats_ref, basis_ref, ortho_ref, upper_ref, scale_ref):
    tile = (8, 128)

    def held(i):
        return jnp.full(tile, stats_ref[i], jnp.float32)

    scale = jnp.sqrt(held(0) / cells + EPS)
    square = scale * scale
    gram = [[held(1 + a * size + b) / cells / square for b in range(size)] for a in range(size)]
    upper = [[None] * size for _ in range(size)]
    for row in range(size):
        value = gram[row][row]
        for prev in range(row):
            value = value - upper[prev][row] * upper[prev][row]
        pivot = jnp.sqrt(value)
        upper[row][row] = pivot
        for col in range(row + 1, size):
            value = gram[row][col]
            for prev in range(row):
                value = value - upper[prev][row] * upper[prev][col]
            upper[row][col] = value / pivot
    inverse = [[None] * size for _ in range(size)]
    for col in range(size):
        for row in reversed(range(col + 1)):
            value = jnp.full(tile, 1.0 if row == col else 0.0, jnp.float32)
            for inner in range(row + 1, col + 1):
                value = value - upper[row][inner] * inverse[inner][col]
            inverse[row][col] = value / upper[row][row]
    rows = lax.broadcasted_iota(jnp.int32, tile, 0)
    cols = lax.broadcasted_iota(jnp.int32, tile, 1)
    packed = jnp.zeros(tile, jnp.float32)
    for row in range(size):
        for col in range(row, size):
            packed = jnp.where((rows == row) & (cols == col), upper[row][col], packed)
    upper_ref[...] = packed
    scale_ref[...] = scale
    lanes = basis_ref.shape[-1] // tile[1]
    weight = [
        [jnp.tile(inverse[j][k] / scale, (1, lanes)) if j <= k else None for k in range(size)]
        for j in range(size)
    ]

    def plane(i, carry):
        parts = [basis_ref[j, i] for j in range(size)]
        for k in range(size):
            acc = parts[0] * weight[0][k]
            for j in range(1, k + 1):
                acc = acc + parts[j] * weight[j][k]
            ortho_ref[k, i] = acc
        return carry

    lax.fori_loop(0, basis_ref.shape[1], plane, 0)


def finish(stats, block, cells):
    size = block.shape[0]
    vmem = pl.BlockSpec(memory_space=pltpu.VMEM)
    ortho, upper, scale = pl.pallas_call(
        lambda *refs: finish_kernel(float(cells), size, *refs),
        out_shape=(
            jax.ShapeDtypeStruct(block.shape, jnp.float32),
            jax.ShapeDtypeStruct((8, 128), jnp.float32),
            jax.ShapeDtypeStruct((8, 128), jnp.float32),
        ),
        in_specs=[pl.BlockSpec(memory_space=pltpu.SMEM), vmem],
        out_specs=(vmem, vmem, vmem),
    )(stats, block)
    return ortho, upper[:size, :size], scale[0, 0]


def local(start_field, right_side, accumulation, trans_x, trans_y, trans_z):
    size_x, size_y, size_z = start_field.shape
    cells = size_x * size_y * size_z * lax.axis_size("gx") * lax.axis_size("gy")

    lo_x, hi_both_x, lo_y, hi_both_y = exchange(
        jnp.concatenate([start_field[:1], trans_x[:1]], axis=0),
        start_field[-1:],
        jnp.concatenate([start_field[:, :1], trans_y[:, :1]], axis=1),
        start_field[:, -1:],
    )
    hi_x, plane_x = hi_both_x[:1], hi_both_x[1:]
    hi_y, plane_y = hi_both_y[:, :1], hi_both_y[:, 1:]

    zero_plane = jnp.zeros_like(trans_z[..., :1])
    tx_lo = trans_x
    tx_hi = jnp.concatenate([trans_x[1:], plane_x], axis=0)
    ty_lo = trans_y
    ty_hi = jnp.concatenate([trans_y[:, 1:], plane_y], axis=1)
    tz_lo = trans_z
    tz_hi = jnp.concatenate([trans_z[..., 1:], zero_plane], axis=-1)
    coef = (tx_lo, tx_hi, ty_lo, ty_hi, tz_lo, tz_hi)
    diagonal = accumulation + tx_lo + tx_hi + ty_lo + ty_hi + tz_lo + tz_hi

    total = neighbour_sum(start_field, (lo_x, hi_x, lo_y, hi_y), coef)
    residual0 = right_side - (diagonal * start_field - total)

    vector = residual0
    basis = [vector]
    for step in range(STEPS):
        total = neighbour_sum(vector, field_halo(vector), coef)
        vector = 2.0 * total / diagonal
        basis.append(vector)
    block = jnp.stack(basis)
    local_gram = jnp.einsum("axyz,bxyz->ab", block, block, precision=lax.Precision.HIGHEST)
    squares = jnp.sum(residual0 * residual0)
    stats = jnp.concatenate([squares[None], local_gram.reshape(-1)])
    stats = all_sum(stats)
    ortho, upper, scale = finish(stats, block, cells)
    return (ortho, upper, scale)


def solution(mesh):
    in_specs = (
        P("gx", "gy", None),
        P("gx", "gy", None),
        P("gx", "gy", None),
        P("gx", "gy", None),
        P("gx", "gy", None),
        P("gx", "gy", None),
    )
    out_specs = (P(None, "gx", "gy", None), P(), P())
    return jax.shard_map(local, mesh=mesh, in_specs=in_specs, out_specs=out_specs, check_vma=False)
```

```python
import jax
import jax.numpy as jnp
from jax import lax
from jax.sharding import PartitionSpec as P
from jax.experimental import pallas as pl
from jax.experimental.pallas import tpu as pltpu

STEPS = 4


EPS = 1e-06


def shift_pairs(axis, by):
    peers = lax.axis_size(axis)
    return [(i, i + by) for i in range(peers) if 0 <= i + by < peers]


def deep_halo(packed, depth):
    from_low = lax.ppermute(packed[-depth:], "gx", shift_pairs("gx", 1))
    from_high = lax.ppermute(packed[:depth], "gx", shift_pairs("gx", -1))
    wide = jnp.concatenate([from_low, packed, from_high], axis=0)
    from_low = lax.ppermute(wide[:, -depth:], "gy", shift_pairs("gy", 1))
    from_high = lax.ppermute(wide[:, :depth], "gy", shift_pairs("gy", -1))
    return jnp.concatenate([from_low, wide, from_high], axis=1)


def shift_z(a):
    return jnp.concatenate([a[..., 1:], jnp.zeros_like(a[..., :1])], axis=-1)


def all_sum(x):
    for axis in ("gy", "gx"):
        n = lax.axis_size(axis)
        if n & (n - 1):
            x = lax.psum(x, axis)
            continue
        step = 1
        while step < n:
            x = x + lax.ppermute(x, axis, [(i, i ^ step) for i in range(n)])
            step *= 2
    return x


def finish_kernel(cells, size, stats_ref, basis_ref, ortho_ref, upper_ref, scale_ref):
    tile = (8, 128)

    def held(i):
        return jnp.full(tile, stats_ref[i], jnp.float32)

    scale = jnp.sqrt(held(0) / cells + EPS)
    square = scale * scale
    gram = [[held(1 + a * size + b) / cells / square for b in range(size)] for a in range(size)]
    upper = [[None] * size for _ in range(size)]
    for row in range(size):
        value = gram[row][row]
        for prev in range(row):
            value = value - upper[prev][row] * upper[prev][row]
        pivot = jnp.sqrt(value)
        upper[row][row] = pivot
        for col in range(row + 1, size):
            value = gram[row][col]
            for prev in range(row):
                value = value - upper[prev][row] * upper[prev][col]
            upper[row][col] = value / pivot
    inverse = [[None] * size for _ in range(size)]
    for col in range(size):
        for row in reversed(range(col + 1)):
            value = jnp.full(tile, 1.0 if row == col else 0.0, jnp.float32)
            for inner in range(row + 1, col + 1):
                value = value - upper[row][inner] * inverse[inner][col]
            inverse[row][col] = value / upper[row][row]
    rows = lax.broadcasted_iota(jnp.int32, tile, 0)
    cols = lax.broadcasted_iota(jnp.int32, tile, 1)
    packed = jnp.zeros(tile, jnp.float32)
    for row in range(size):
        for col in range(row, size):
            packed = jnp.where((rows == row) & (cols == col), upper[row][col], packed)
    upper_ref[...] = packed
    scale_ref[...] = scale
    lanes = basis_ref.shape[-1] // tile[1]
    weight = [
        [jnp.tile(inverse[j][k] / scale, (1, lanes)) if j <= k else None for k in range(size)]
        for j in range(size)
    ]

    def plane(i, carry):
        parts = [basis_ref[j, i] for j in range(size)]
        for k in range(size):
            acc = parts[0] * weight[0][k]
            for j in range(1, k + 1):
                acc = acc + parts[j] * weight[j][k]
            ortho_ref[k, i] = acc
        return carry

    lax.fori_loop(0, basis_ref.shape[1], plane, 0)


def finish(stats, block, cells):
    size = block.shape[0]
    vmem = pl.BlockSpec(memory_space=pltpu.VMEM)
    ortho, upper, scale = pl.pallas_call(
        lambda *refs: finish_kernel(float(cells), size, *refs),
        out_shape=(
            jax.ShapeDtypeStruct(block.shape, jnp.float32),
            jax.ShapeDtypeStruct((8, 128), jnp.float32),
            jax.ShapeDtypeStruct((8, 128), jnp.float32),
        ),
        in_specs=[pl.BlockSpec(memory_space=pltpu.SMEM), vmem],
        out_specs=(vmem, vmem, vmem),
    )(stats, block)
    return ortho, upper[:size, :size], scale[0, 0]


def local(start_field, right_side, accumulation, trans_x, trans_y, trans_z):
    size_x, size_y, size_z = start_field.shape
    cells = size_x * size_y * size_z * lax.axis_size("gx") * lax.axis_size("gy")
    depth = STEPS + 1

    inputs = (start_field, right_side, accumulation, trans_x, trans_y, trans_z)
    wide = deep_halo(jnp.concatenate(inputs, axis=-1), depth)
    field, rhs, acc, t_x, t_y, t_z = (wide[..., k * size_z : (k + 1) * size_z] for k in range(len(inputs)))

    first_x = lax.axis_index("gx") * size_x - depth
    first_y = lax.axis_index("gy") * size_y - depth
    grid_x = size_x * lax.axis_size("gx")
    grid_y = size_y * lax.axis_size("gy")

    def region(a, m, dx=0, dy=0):
        o = depth - m
        return a[o + dx : o + dx + size_x + 2 * m, o + dy : o + dy + size_y + 2 * m]

    def inside(m):
        o = depth - m
        gi = first_x + o + lax.broadcasted_iota(jnp.int32, (size_x + 2 * m, 1, 1), 0)
        gj = first_y + o + lax.broadcasted_iota(jnp.int32, (1, size_y + 2 * m, 1), 1)
        return (gi >= 0) & (gi < grid_x) & (gj >= 0) & (gj < grid_y)

    def coefficients(m):
        tz_lo = region(t_z, m)
        return (region(t_x, m), region(t_x, m, 1), region(t_y, m), region(t_y, m, 0, 1), tz_lo, shift_z(tz_lo))

    def neighbour_sum(u, coef):
        tx_lo, tx_hi, ty_lo, ty_hi, tz_lo, tz_hi = coef
        centre = u[1:-1, 1:-1]
        zero_plane = jnp.zeros_like(centre[..., :1])
        z_low = jnp.concatenate([zero_plane, centre[..., :-1]], axis=-1)
        z_high = jnp.concatenate([centre[..., 1:], zero_plane], axis=-1)
        total = tx_lo * u[:-2, 1:-1] + tx_hi * u[2:, 1:-1]
        total = total + ty_lo * u[1:-1, :-2] + ty_hi * u[1:-1, 2:]
        total = total + tz_lo * z_low + tz_hi * z_high
        return total

    coef = coefficients(STEPS)
    tx_lo, tx_hi, ty_lo, ty_hi, tz_lo, tz_hi = coef
    diagonal = region(acc, STEPS) + tx_lo + tx_hi + ty_lo + ty_hi + tz_lo + tz_hi
    total = neighbour_sum(field, coef)
    residual0 = region(rhs, STEPS) - (diagonal * region(field, STEPS) - total)
    vector = jnp.where(inside(STEPS), residual0, 0.0)

    basis = [vector[STEPS : STEPS + size_x, STEPS : STEPS + size_y]]
    for step in range(STEPS):
        m = STEPS - 1 - step
        cut = STEPS - m
        total = neighbour_sum(vector, coefficients(m))
        vector = 2.0 * total / diagonal[cut : cut + size_x + 2 * m, cut : cut + size_y + 2 * m]
        if m:
            vector = jnp.where(inside(m), vector, 0.0)
        basis.append(vector[m : m + size_x, m : m + size_y])
    block = jnp.stack(basis)
    local_gram = jnp.einsum("axyz,bxyz->ab", block, block, precision=lax.Precision.HIGHEST)
    squares = jnp.sum(basis[0] * basis[0])
    stats = jnp.concatenate([squares[None], local_gram.reshape(-1)])
    stats = all_sum(stats)
    ortho, upper, scale = finish(stats, block, cells)
    return (ortho, upper, scale)


def solution(mesh):
    in_specs = (
        P("gx", "gy", None),
        P("gx", "gy", None),
        P("gx", "gy", None),
        P("gx", "gy", None),
        P("gx", "gy", None),
        P("gx", "gy", None),
    )
    out_specs = (P(None, "gx", "gy", None), P(), P())
    return jax.shard_map(local, mesh=mesh, in_specs=in_specs, out_specs=out_specs, check_vma=False)
```

```python
import jax
import jax.numpy as jnp
from jax import lax
from jax.sharding import PartitionSpec as P
from jax.experimental import pallas as pl
from jax.experimental.pallas import tpu as pltpu

STEPS = 4


EPS = 1e-06


def shift_pairs(axis, by):
    peers = lax.axis_size(axis)
    return [(i, i + by) for i in range(peers) if 0 <= i + by < peers]


def swap_pairs(axis, parity):
    peers = lax.axis_size(axis)
    pairs = []
    for i in range(parity, peers - 1, 2):
        pairs += [(i, i + 1), (i + 1, i)]
    return pairs


def axis_exchange(to_low, to_high, axis):
    odd = lax.axis_index(axis) % 2 == 1
    even_swap = lax.ppermute(jnp.where(odd, to_low, to_high), axis, swap_pairs(axis, 0))
    odd_swap = lax.ppermute(jnp.where(odd, to_high, to_low), axis, swap_pairs(axis, 1))
    from_low = jnp.where(odd, even_swap, odd_swap)
    from_high = jnp.where(odd, odd_swap, even_swap)
    return from_low, from_high


def exchange(to_low_x, to_high_x, to_low_y, to_high_y):
    from_low_x, from_high_x = axis_exchange(to_low_x, to_high_x, "gx")
    from_low_y, from_high_y = axis_exchange(to_low_y, to_high_y, "gy")
    return from_low_x, from_high_x, from_low_y, from_high_y


def neighbour_sum(u, halo, coef):
    lo_x, hi_x, lo_y, hi_y = halo
    tx_lo, tx_hi, ty_lo, ty_hi, tz_lo, tz_hi = coef
    zero_plane = jnp.zeros_like(u[..., :1])
    u_xm = jnp.concatenate([lo_x, u[:-1]], axis=0)
    u_xp = jnp.concatenate([u[1:], hi_x], axis=0)
    u_ym = jnp.concatenate([lo_y, u[:, :-1]], axis=1)
    u_yp = jnp.concatenate([u[:, 1:], hi_y], axis=1)
    u_zm = jnp.concatenate([zero_plane, u[..., :-1]], axis=-1)
    u_zp = jnp.concatenate([u[..., 1:], zero_plane], axis=-1)
    total = tx_lo * u_xm + tx_hi * u_xp
    total = total + ty_lo * u_ym + ty_hi * u_yp
    total = total + tz_lo * u_zm + tz_hi * u_zp
    return total


def field_halo(u):
    return exchange(u[:1], u[-1:], u[:, :1], u[:, -1:])


def all_sum(x):
    for axis in ("gy", "gx"):
        n = lax.axis_size(axis)
        if n & (n - 1):
            x = lax.psum(x, axis)
            continue
        step = 1
        while step < n:
            x = x + lax.ppermute(x, axis, [(i, i ^ step) for i in range(n)])
            step *= 2
    return x


def finish_kernel(cells, size, stats_ref, basis_ref, ortho_ref, upper_ref, scale_ref):
    tile = (8, 128)

    def held(i):
        return jnp.full(tile, stats_ref[i], jnp.float32)

    scale = jnp.sqrt(held(0) / cells + EPS)
    square = scale * scale
    gram = [[held(1 + a * size + b) / cells / square for b in range(size)] for a in range(size)]
    upper = [[None] * size for _ in range(size)]
    for row in range(size):
        value = gram[row][row]
        for prev in range(row):
            value = value - upper[prev][row] * upper[prev][row]
        pivot = jnp.sqrt(value)
        upper[row][row] = pivot
        for col in range(row + 1, size):
            value = gram[row][col]
            for prev in range(row):
                value = value - upper[prev][row] * upper[prev][col]
            upper[row][col] = value / pivot
    inverse = [[None] * size for _ in range(size)]
    for col in range(size):
        for row in reversed(range(col + 1)):
            value = jnp.full(tile, 1.0 if row == col else 0.0, jnp.float32)
            for inner in range(row + 1, col + 1):
                value = value - upper[row][inner] * inverse[inner][col]
            inverse[row][col] = value / upper[row][row]
    rows = lax.broadcasted_iota(jnp.int32, tile, 0)
    cols = lax.broadcasted_iota(jnp.int32, tile, 1)
    packed = jnp.zeros(tile, jnp.float32)
    for row in range(size):
        for col in range(row, size):
            packed = jnp.where((rows == row) & (cols == col), upper[row][col], packed)
    upper_ref[...] = packed
    scale_ref[...] = scale
    lanes = basis_ref.shape[-1] // tile[1]
    weight = [
        [jnp.tile(inverse[j][k] / scale, (1, lanes)) if j <= k else None for k in range(size)]
        for j in range(size)
    ]

    def plane(i, carry):
        parts = [basis_ref[j, i] for j in range(size)]
        for k in range(size):
            acc = parts[0] * weight[0][k]
            for j in range(1, k + 1):
                acc = acc + parts[j] * weight[j][k]
            ortho_ref[k, i] = acc
        return carry

    lax.fori_loop(0, basis_ref.shape[1], plane, 0)


def finish(stats, block, cells):
    size = block.shape[0]
    vmem = pl.BlockSpec(memory_space=pltpu.VMEM)
    ortho, upper, scale = pl.pallas_call(
        lambda *refs: finish_kernel(float(cells), size, *refs),
        out_shape=(
            jax.ShapeDtypeStruct(block.shape, jnp.float32),
            jax.ShapeDtypeStruct((8, 128), jnp.float32),
            jax.ShapeDtypeStruct((8, 128), jnp.float32),
        ),
        in_specs=[pl.BlockSpec(memory_space=pltpu.SMEM), vmem],
        out_specs=(vmem, vmem, vmem),
    )(stats, block)
    return ortho, upper[:size, :size], scale[0, 0]


def local(start_field, right_side, accumulation, trans_x, trans_y, trans_z):
    size_x, size_y, size_z = start_field.shape
    cells = size_x * size_y * size_z * lax.axis_size("gx") * lax.axis_size("gy")

    lo_both_x, hi_both_x, lo_both_y, hi_both_y = exchange(
        jnp.concatenate([start_field[:1], trans_x[:1]], axis=0),
        jnp.concatenate([start_field[-1:], trans_x[-1:]], axis=0),
        jnp.concatenate([start_field[:, :1], trans_y[:, :1]], axis=1),
        jnp.concatenate([start_field[:, -1:], trans_y[:, -1:]], axis=1),
    )
    lo_x, hi_x, plane_x = lo_both_x[:1], hi_both_x[:1], hi_both_x[1:]
    lo_y, hi_y, plane_y = lo_both_y[:, :1], hi_both_y[:, :1], hi_both_y[:, 1:]

    zero_plane = jnp.zeros_like(trans_z[..., :1])
    tx_lo = trans_x
    tx_hi = jnp.concatenate([trans_x[1:], plane_x], axis=0)
    ty_lo = trans_y
    ty_hi = jnp.concatenate([trans_y[:, 1:], plane_y], axis=1)
    tz_lo = trans_z
    tz_hi = jnp.concatenate([trans_z[..., 1:], zero_plane], axis=-1)
    coef = (tx_lo, tx_hi, ty_lo, ty_hi, tz_lo, tz_hi)
    diagonal = accumulation + tx_lo + tx_hi + ty_lo + ty_hi + tz_lo + tz_hi

    total = neighbour_sum(start_field, (lo_x, hi_x, lo_y, hi_y), coef)
    residual0 = right_side - (diagonal * start_field - total)

    vector = residual0
    basis = [vector]
    for step in range(STEPS):
        total = neighbour_sum(vector, field_halo(vector), coef)
        vector = 2.0 * total / diagonal
        basis.append(vector)
    block = jnp.stack(basis)
    local_gram = jnp.einsum("axyz,bxyz->ab", block, block, precision=lax.Precision.HIGHEST)
    squares = jnp.sum(residual0 * residual0)
    stats = jnp.concatenate([squares[None], local_gram.reshape(-1)])
    stats = all_sum(stats)
    ortho, upper, scale = finish(stats, block, cells)
    return (ortho, upper, scale)


def solution(mesh):
    in_specs = (
        P("gx", "gy", None),
        P("gx", "gy", None),
        P("gx", "gy", None),
        P("gx", "gy", None),
        P("gx", "gy", None),
        P("gx", "gy", None),
    )
    out_specs = (P(None, "gx", "gy", None), P(), P())
    return jax.shard_map(local, mesh=mesh, in_specs=in_specs, out_specs=out_specs, check_vma=False)
```

```python
import jax
import jax.numpy as jnp
from jax import lax
from jax.sharding import PartitionSpec as P
from jax.experimental import pallas as pl
from jax.experimental.pallas import tpu as pltpu

STEPS = 4


EPS = 1e-06


def shift_pairs(axis, by):
    peers = lax.axis_size(axis)
    return [(i, i + by) for i in range(peers) if 0 <= i + by < peers]


def swap_pairs(axis, parity):
    peers = lax.axis_size(axis)
    pairs = []
    for i in range(parity, peers - 1, 2):
        pairs += [(i, i + 1), (i + 1, i)]
    return pairs


def axis_exchange(to_low, to_high, axis):
    odd = lax.axis_index(axis) % 2 == 1
    even_swap = lax.ppermute(jnp.where(odd, to_low, to_high), axis, swap_pairs(axis, 0))
    odd_swap = lax.ppermute(jnp.where(odd, to_high, to_low), axis, swap_pairs(axis, 1))
    from_low = jnp.where(odd, even_swap, odd_swap)
    from_high = jnp.where(odd, odd_swap, even_swap)
    return from_low, from_high


def exchange(to_low_x, to_high_x, to_low_y, to_high_y):
    from_low_x, from_high_x = axis_exchange(to_low_x, to_high_x, "gx")
    from_low_y, from_high_y = axis_exchange(to_low_y, to_high_y, "gy")
    return from_low_x, from_high_x, from_low_y, from_high_y


def neighbour_sum(u, halo, coef):
    lo_x, hi_x, lo_y, hi_y = halo
    tx_lo, tx_hi, ty_lo, ty_hi, tz_lo, tz_hi = coef
    zero_plane = jnp.zeros_like(u[..., :1])
    u_xm = jnp.concatenate([lo_x, u[:-1]], axis=0)
    u_xp = jnp.concatenate([u[1:], hi_x], axis=0)
    u_ym = jnp.concatenate([lo_y, u[:, :-1]], axis=1)
    u_yp = jnp.concatenate([u[:, 1:], hi_y], axis=1)
    u_zm = jnp.concatenate([zero_plane, u[..., :-1]], axis=-1)
    u_zp = jnp.concatenate([u[..., 1:], zero_plane], axis=-1)
    total = tx_lo * u_xm + tx_hi * u_xp
    total = total + ty_lo * u_ym + ty_hi * u_yp
    total = total + tz_lo * u_zm + tz_hi * u_zp
    return total


def field_halo(u):
    return exchange(u[:1], u[-1:], u[:, :1], u[:, -1:])


def all_sum(x):
    for axis in ("gy", "gx"):
        n = lax.axis_size(axis)
        if n & (n - 1):
            x = lax.psum(x, axis)
            continue
        step = 1
        while step < n:
            x = x + lax.ppermute(x, axis, [(i, i ^ step) for i in range(n)])
            step *= 2
    return x


def finish_kernel(cells, size, stats_ref, basis_ref, ortho_ref, upper_ref, scale_ref):
    tile = (8, 128)

    def held(i):
        return jnp.full(tile, stats_ref[i], jnp.float32)

    scale = jnp.sqrt(held(0) / cells + EPS)
    square = scale * scale
    gram = [[held(1 + a * size + b) / cells / square for b in range(size)] for a in range(size)]
    upper = [[None] * size for _ in range(size)]
    for row in range(size):
        value = gram[row][row]
        for prev in range(row):
            value = value - upper[prev][row] * upper[prev][row]
        pivot = jnp.sqrt(value)
        upper[row][row] = pivot
        for col in range(row + 1, size):
            value = gram[row][col]
            for prev in range(row):
                value = value - upper[prev][row] * upper[prev][col]
            upper[row][col] = value / pivot
    inverse = [[None] * size for _ in range(size)]
    for col in range(size):
        for row in reversed(range(col + 1)):
            value = jnp.full(tile, 1.0 if row == col else 0.0, jnp.float32)
            for inner in range(row + 1, col + 1):
                value = value - upper[row][inner] * inverse[inner][col]
            inverse[row][col] = value / upper[row][row]
    rows = lax.broadcasted_iota(jnp.int32, tile, 0)
    cols = lax.broadcasted_iota(jnp.int32, tile, 1)
    packed = jnp.zeros(tile, jnp.float32)
    for row in range(size):
        for col in range(row, size):
            packed = jnp.where((rows == row) & (cols == col), upper[row][col], packed)
    upper_ref[...] = packed[: upper_ref.shape[0], : upper_ref.shape[1]]
    scale_ref[...] = scale[:1, :1]
    lanes = basis_ref.shape[-1] // tile[1]
    weight = [
        [jnp.tile(inverse[j][k] / scale, (1, lanes)) if j <= k else None for k in range(size)]
        for j in range(size)
    ]

    def plane(i, carry):
        parts = [basis_ref[j, i] for j in range(size)]
        for k in range(size):
            acc = parts[0] * weight[0][k]
            for j in range(1, k + 1):
                acc = acc + parts[j] * weight[j][k]
            ortho_ref[k, i] = acc
        return carry

    lax.fori_loop(0, basis_ref.shape[1], plane, 0)


def finish(stats, block, cells):
    size = block.shape[0]
    vmem = pl.BlockSpec(memory_space=pltpu.VMEM)
    ortho, upper, scale = pl.pallas_call(
        lambda *refs: finish_kernel(float(cells), size, *refs),
        out_shape=(
            jax.ShapeDtypeStruct(block.shape, jnp.float32),
            jax.ShapeDtypeStruct((size, size), jnp.float32),
            jax.ShapeDtypeStruct((1, 1), jnp.float32),
        ),
        in_specs=[pl.BlockSpec(memory_space=pltpu.SMEM), vmem],
        out_specs=(vmem, vmem, vmem),
    )(stats, block)
    return ortho, upper, scale.reshape(())


def local(start_field, right_side, accumulation, trans_x, trans_y, trans_z):
    size_x, size_y, size_z = start_field.shape
    cells = size_x * size_y * size_z * lax.axis_size("gx") * lax.axis_size("gy")

    lo_both_x, hi_both_x, lo_both_y, hi_both_y = exchange(
        jnp.concatenate([start_field[:1], trans_x[:1]], axis=0),
        jnp.concatenate([start_field[-1:], trans_x[-1:]], axis=0),
        jnp.concatenate([start_field[:, :1], trans_y[:, :1]], axis=1),
        jnp.concatenate([start_field[:, -1:], trans_y[:, -1:]], axis=1),
    )
    lo_x, hi_x, plane_x = lo_both_x[:1], hi_both_x[:1], hi_both_x[1:]
    lo_y, hi_y, plane_y = lo_both_y[:, :1], hi_both_y[:, :1], hi_both_y[:, 1:]

    zero_plane = jnp.zeros_like(trans_z[..., :1])
    tx_lo = trans_x
    tx_hi = jnp.concatenate([trans_x[1:], plane_x], axis=0)
    ty_lo = trans_y
    ty_hi = jnp.concatenate([trans_y[:, 1:], plane_y], axis=1)
    tz_lo = trans_z
    tz_hi = jnp.concatenate([trans_z[..., 1:], zero_plane], axis=-1)
    coef = (tx_lo, tx_hi, ty_lo, ty_hi, tz_lo, tz_hi)
    diagonal = accumulation + tx_lo + tx_hi + ty_lo + ty_hi + tz_lo + tz_hi

    total = neighbour_sum(start_field, (lo_x, hi_x, lo_y, hi_y), coef)
    residual0 = right_side - (diagonal * start_field - total)

    vector = residual0
    basis = [vector]
    gram_rows = [[jnp.sum(vector * vector)]]
    for step in range(STEPS):
        total = neighbour_sum(vector, field_halo(vector), coef)
        vector = 2.0 * total / diagonal
        gram_rows.append([jnp.sum(vector * earlier) for earlier in basis] + [jnp.sum(vector * vector)])
        basis.append(vector)
    block = jnp.stack(basis)
    size = len(basis)
    local_gram = [[gram_rows[max(a, b)][min(a, b)] for b in range(size)] for a in range(size)]
    squares = gram_rows[0][0]
    stats = jnp.stack([squares] + [entry for row in local_gram for entry in row])
    stats = all_sum(stats)
    ortho, upper, scale = finish(stats, block, cells)
    return (ortho, upper, scale)


def solution(mesh):
    in_specs = (
        P("gx", "gy", None),
        P("gx", "gy", None),
        P("gx", "gy", None),
        P("gx", "gy", None),
        P("gx", "gy", None),
        P("gx", "gy", None),
    )
    out_specs = (P(None, "gx", "gy", None), P(), P())
    return jax.shard_map(local, mesh=mesh, in_specs=in_specs, out_specs=out_specs, check_vma=False)
```

```python
import jax
import jax.numpy as jnp
from jax import lax
from jax.sharding import PartitionSpec as P
from jax.experimental import pallas as pl
from jax.experimental.pallas import tpu as pltpu

STEPS = 4


EPS = 1e-06


def shift_pairs(axis, by):
    peers = lax.axis_size(axis)
    return [(i, i + by) for i in range(peers) if 0 <= i + by < peers]


def swap_pairs(axis, parity):
    peers = lax.axis_size(axis)
    pairs = []
    for i in range(parity, peers - 1, 2):
        pairs += [(i, i + 1), (i + 1, i)]
    return pairs


def axis_exchange(to_low, to_high, axis):
    odd = lax.axis_index(axis) % 2 == 1
    even_swap = lax.ppermute(jnp.where(odd, to_low, to_high), axis, swap_pairs(axis, 0))
    odd_swap = lax.ppermute(jnp.where(odd, to_high, to_low), axis, swap_pairs(axis, 1))
    from_low = jnp.where(odd, even_swap, odd_swap)
    from_high = jnp.where(odd, odd_swap, even_swap)
    return from_low, from_high


def exchange(to_low_x, to_high_x, to_low_y, to_high_y):
    from_low_x, from_high_x = axis_exchange(to_low_x, to_high_x, "gx")
    from_low_y, from_high_y = axis_exchange(to_low_y, to_high_y, "gy")
    return from_low_x, from_high_x, from_low_y, from_high_y


def neighbour_sum(u, halo, coef):
    lo_x, hi_x, lo_y, hi_y = halo
    tx_lo, tx_hi, ty_lo, ty_hi, tz_lo, tz_hi = coef
    zero_plane = jnp.zeros_like(u[..., :1])
    u_xm = jnp.concatenate([lo_x, u[:-1]], axis=0)
    u_xp = jnp.concatenate([u[1:], hi_x], axis=0)
    u_ym = jnp.concatenate([lo_y, u[:, :-1]], axis=1)
    u_yp = jnp.concatenate([u[:, 1:], hi_y], axis=1)
    u_zm = jnp.concatenate([zero_plane, u[..., :-1]], axis=-1)
    u_zp = jnp.concatenate([u[..., 1:], zero_plane], axis=-1)
    total = tx_lo * u_xm + tx_hi * u_xp
    total = total + ty_lo * u_ym + ty_hi * u_yp
    total = total + tz_lo * u_zm + tz_hi * u_zp
    return total


def field_halo(u):
    return exchange(u[:1], u[-1:], u[:, :1], u[:, -1:])


def all_sum(x):
    for axis in ("gy", "gx"):
        n = lax.axis_size(axis)
        if n & (n - 1):
            x = lax.psum(x, axis)
            continue
        step = 1
        while step < n:
            x = x + lax.ppermute(x, axis, [(i, i ^ step) for i in range(n)])
            step *= 2
    return x


def gram_kernel(size, *refs):
    basis_refs, out_ref = refs[:size], refs[size]
    tile = out_ref.shape
    pairs = [(a, b) for a in range(size) for b in range(a, size)]
    planes, rows, lanes = basis_refs[0].shape
    chunks = lanes // tile[1]

    def plane(i, accs):
        accs = list(accs)
        for c in range(chunks):
            parts = [r[i, :, c * tile[1] : (c + 1) * tile[1]] for r in basis_refs]
            for n, (a, b) in enumerate(pairs):
                accs[n] = accs[n] + parts[a] * parts[b]
        return tuple(accs)

    zero = jnp.zeros((rows, tile[1]), jnp.float32)
    accs = lax.fori_loop(0, planes, plane, tuple(zero for _ in pairs))
    row_ids = lax.broadcasted_iota(jnp.int32, tile, 0)
    lane_ids = lax.broadcasted_iota(jnp.int32, tile, 1)
    packed = jnp.zeros(tile, jnp.float32)
    for n, (a, b) in enumerate(pairs):
        total = jnp.sum(accs[n])
        hit = (lane_ids == 1 + a * size + b) | (lane_ids == 1 + b * size + a)
        if a == 0 and b == 0:
            hit = hit | (lane_ids == 0)
        packed = jnp.where((row_ids == 0) & hit, total, packed)
    out_ref[...] = packed


def gram(basis):
    size = len(basis)
    vmem = pl.BlockSpec(memory_space=pltpu.VMEM)
    return pl.pallas_call(
        lambda *refs: gram_kernel(size, *refs),
        out_shape=jax.ShapeDtypeStruct((8, 128), jnp.float32),
        in_specs=[vmem] * size,
        out_specs=vmem,
    )(*basis)


def finish_kernel(cells, size, stats_ref, *refs):
    basis_refs, (ortho_ref, upper_ref, scale_ref) = refs[:size], refs[size:]
    tile = (8, 128)

    def held(i):
        return jnp.full(tile, stats_ref[0, i], jnp.float32)

    scale = jnp.sqrt(held(0) / cells + EPS)
    square = scale * scale
    gram = [[held(1 + a * size + b) / cells / square for b in range(size)] for a in range(size)]
    upper = [[None] * size for _ in range(size)]
    for row in range(size):
        value = gram[row][row]
        for prev in range(row):
            value = value - upper[prev][row] * upper[prev][row]
        pivot = jnp.sqrt(value)
        upper[row][row] = pivot
        for col in range(row + 1, size):
            value = gram[row][col]
            for prev in range(row):
                value = value - upper[prev][row] * upper[prev][col]
            upper[row][col] = value / pivot
    inverse = [[None] * size for _ in range(size)]
    for col in range(size):
        for row in reversed(range(col + 1)):
            value = jnp.full(tile, 1.0 if row == col else 0.0, jnp.float32)
            for inner in range(row + 1, col + 1):
                value = value - upper[row][inner] * inverse[inner][col]
            inverse[row][col] = value / upper[row][row]
    rows = lax.broadcasted_iota(jnp.int32, tile, 0)
    cols = lax.broadcasted_iota(jnp.int32, tile, 1)
    packed = jnp.zeros(tile, jnp.float32)
    for row in range(size):
        for col in range(row, size):
            packed = jnp.where((rows == row) & (cols == col), upper[row][col], packed)
    upper_ref[...] = packed[: upper_ref.shape[0], : upper_ref.shape[1]]
    scale_ref[...] = scale[:1, :1]
    lanes = basis_refs[0].shape[-1] // tile[1]
    weight = [
        [jnp.tile(inverse[j][k] / scale, (1, lanes)) if j <= k else None for k in range(size)]
        for j in range(size)
    ]

    def plane(i, carry):
        parts = [basis_refs[j][i] for j in range(size)]
        for k in range(size):
            acc = parts[0] * weight[0][k]
            for j in range(1, k + 1):
                acc = acc + parts[j] * weight[j][k]
            ortho_ref[k, i] = acc
        return carry

    lax.fori_loop(0, basis_refs[0].shape[0], plane, 0)


def finish(stats, basis, cells):
    size = len(basis)
    vmem = pl.BlockSpec(memory_space=pltpu.VMEM)
    ortho, upper, scale = pl.pallas_call(
        lambda *refs: finish_kernel(float(cells), size, *refs),
        out_shape=(
            jax.ShapeDtypeStruct((size,) + basis[0].shape, jnp.float32),
            jax.ShapeDtypeStruct((size, size), jnp.float32),
            jax.ShapeDtypeStruct((1, 1), jnp.float32),
        ),
        in_specs=[pl.BlockSpec(memory_space=pltpu.SMEM)] + [vmem] * size,
        out_specs=(vmem, vmem, vmem),
    )(stats, *basis)
    return ortho, upper, scale.reshape(())


def local(start_field, right_side, accumulation, trans_x, trans_y, trans_z):
    size_x, size_y, size_z = start_field.shape
    cells = size_x * size_y * size_z * lax.axis_size("gx") * lax.axis_size("gy")

    lo_both_x, hi_both_x, lo_both_y, hi_both_y = exchange(
        jnp.concatenate([start_field[:1], trans_x[:1]], axis=0),
        jnp.concatenate([start_field[-1:], trans_x[-1:]], axis=0),
        jnp.concatenate([start_field[:, :1], trans_y[:, :1]], axis=1),
        jnp.concatenate([start_field[:, -1:], trans_y[:, -1:]], axis=1),
    )
    lo_x, hi_x, plane_x = lo_both_x[:1], hi_both_x[:1], hi_both_x[1:]
    lo_y, hi_y, plane_y = lo_both_y[:, :1], hi_both_y[:, :1], hi_both_y[:, 1:]

    zero_plane = jnp.zeros_like(trans_z[..., :1])
    tx_lo = trans_x
    tx_hi = jnp.concatenate([trans_x[1:], plane_x], axis=0)
    ty_lo = trans_y
    ty_hi = jnp.concatenate([trans_y[:, 1:], plane_y], axis=1)
    tz_lo = trans_z
    tz_hi = jnp.concatenate([trans_z[..., 1:], zero_plane], axis=-1)
    coef = (tx_lo, tx_hi, ty_lo, ty_hi, tz_lo, tz_hi)
    diagonal = accumulation + tx_lo + tx_hi + ty_lo + ty_hi + tz_lo + tz_hi

    total = neighbour_sum(start_field, (lo_x, hi_x, lo_y, hi_y), coef)
    residual0 = right_side - (diagonal * start_field - total)

    vector = residual0
    basis = [vector]
    for step in range(STEPS):
        total = neighbour_sum(vector, field_halo(vector), coef)
        vector = 2.0 * total / diagonal
        basis.append(vector)
    stats = gram(basis)
    stats = all_sum(stats)
    ortho, upper, scale = finish(stats, basis, cells)
    return (ortho, upper, scale)


def solution(mesh):
    in_specs = (
        P("gx", "gy", None),
        P("gx", "gy", None),
        P("gx", "gy", None),
        P("gx", "gy", None),
        P("gx", "gy", None),
        P("gx", "gy", None),
    )
    out_specs = (P(None, "gx", "gy", None), P(), P())
    return jax.shard_map(local, mesh=mesh, in_specs=in_specs, out_specs=out_specs, check_vma=False)
```

```python
import jax
import jax.numpy as jnp
from jax import lax
from jax.sharding import PartitionSpec as P
from jax.experimental import pallas as pl
from jax.experimental.pallas import tpu as pltpu

STEPS = 4


EPS = 1e-06


def shift_pairs(axis, by):
    peers = lax.axis_size(axis)
    return [(i, i + by) for i in range(peers) if 0 <= i + by < peers]


def swap_pairs(axis, parity):
    peers = lax.axis_size(axis)
    pairs = []
    for i in range(parity, peers - 1, 2):
        pairs += [(i, i + 1), (i + 1, i)]
    return pairs


def axis_exchange(to_low, to_high, axis):
    odd = lax.axis_index(axis) % 2 == 1
    even_swap = lax.ppermute(jnp.where(odd, to_low, to_high), axis, swap_pairs(axis, 0))
    odd_swap = lax.ppermute(jnp.where(odd, to_high, to_low), axis, swap_pairs(axis, 1))
    from_low = jnp.where(odd, even_swap, odd_swap)
    from_high = jnp.where(odd, odd_swap, even_swap)
    return from_low, from_high


def exchange(to_low_x, to_high_x, to_low_y, to_high_y):
    from_low_x, from_high_x = axis_exchange(to_low_x, to_high_x, "gx")
    from_low_y, from_high_y = axis_exchange(to_low_y, to_high_y, "gy")
    return from_low_x, from_high_x, from_low_y, from_high_y


def neighbour_sum(u, halo, coef):
    lo_x, hi_x, lo_y, hi_y = halo
    tx_lo, tx_hi, ty_lo, ty_hi, tz_lo, tz_hi = coef
    zero_plane = jnp.zeros_like(u[..., :1])
    u_xm = jnp.concatenate([lo_x, u[:-1]], axis=0)
    u_xp = jnp.concatenate([u[1:], hi_x], axis=0)
    u_ym = jnp.concatenate([lo_y, u[:, :-1]], axis=1)
    u_yp = jnp.concatenate([u[:, 1:], hi_y], axis=1)
    u_zm = jnp.concatenate([zero_plane, u[..., :-1]], axis=-1)
    u_zp = jnp.concatenate([u[..., 1:], zero_plane], axis=-1)
    total = tx_lo * u_xm + tx_hi * u_xp
    total = total + ty_lo * u_ym + ty_hi * u_yp
    total = total + tz_lo * u_zm + tz_hi * u_zp
    return total


def field_halo(u):
    return exchange(u[:1], u[-1:], u[:, :1], u[:, -1:])


def shift_z(a):
    return jnp.concatenate([a[..., 1:], jnp.zeros_like(a[..., :1])], axis=-1)


def all_sum(x):
    for axis in ("gy", "gx"):
        n = lax.axis_size(axis)
        if n & (n - 1):
            x = lax.psum(x, axis)
            continue
        step = 1
        while step < n:
            x = x + lax.ppermute(x, axis, [(i, i ^ step) for i in range(n)])
            step *= 2
    return x


def gram_kernel(size, *refs):
    basis_refs, out_ref = refs[:size], refs[size]
    tile = out_ref.shape
    pairs = [(a, b) for a in range(size) for b in range(a, size)]
    planes, rows, lanes = basis_refs[0].shape
    chunks = lanes // tile[1]

    def plane(i, accs):
        accs = list(accs)
        for c in range(chunks):
            parts = [r[i, :, c * tile[1] : (c + 1) * tile[1]] for r in basis_refs]
            for n, (a, b) in enumerate(pairs):
                accs[n] = accs[n] + parts[a] * parts[b]
        return tuple(accs)

    zero = jnp.zeros((rows, tile[1]), jnp.float32)
    accs = lax.fori_loop(0, planes, plane, tuple(zero for _ in pairs))
    row_ids = lax.broadcasted_iota(jnp.int32, tile, 0)
    lane_ids = lax.broadcasted_iota(jnp.int32, tile, 1)
    packed = jnp.zeros(tile, jnp.float32)
    for n, (a, b) in enumerate(pairs):
        total = jnp.sum(accs[n])
        hit = (lane_ids == 1 + a * size + b) | (lane_ids == 1 + b * size + a)
        if a == 0 and b == 0:
            hit = hit | (lane_ids == 0)
        packed = jnp.where((row_ids == 0) & hit, total, packed)
    out_ref[...] = packed


def gram(basis):
    size = len(basis)
    vmem = pl.BlockSpec(memory_space=pltpu.VMEM)
    return pl.pallas_call(
        lambda *refs: gram_kernel(size, *refs),
        out_shape=jax.ShapeDtypeStruct((8, 128), jnp.float32),
        in_specs=[vmem] * size,
        out_specs=vmem,
    )(*basis)


def finish_kernel(cells, size, stats_ref, *refs):
    basis_refs, (ortho_ref, upper_ref, scale_ref) = refs[:size], refs[size:]
    tile = (8, 128)

    def held(i):
        return jnp.full(tile, stats_ref[0, i], jnp.float32)

    scale = jnp.sqrt(held(0) / cells + EPS)
    square = scale * scale
    gram = [[held(1 + a * size + b) / cells / square for b in range(size)] for a in range(size)]
    upper = [[None] * size for _ in range(size)]
    for row in range(size):
        value = gram[row][row]
        for prev in range(row):
            value = value - upper[prev][row] * upper[prev][row]
        pivot = jnp.sqrt(value)
        upper[row][row] = pivot
        for col in range(row + 1, size):
            value = gram[row][col]
            for prev in range(row):
                value = value - upper[prev][row] * upper[prev][col]
            upper[row][col] = value / pivot
    inverse = [[None] * size for _ in range(size)]
    for col in range(size):
        for row in reversed(range(col + 1)):
            value = jnp.full(tile, 1.0 if row == col else 0.0, jnp.float32)
            for inner in range(row + 1, col + 1):
                value = value - upper[row][inner] * inverse[inner][col]
            inverse[row][col] = value / upper[row][row]
    rows = lax.broadcasted_iota(jnp.int32, tile, 0)
    cols = lax.broadcasted_iota(jnp.int32, tile, 1)
    packed = jnp.zeros(tile, jnp.float32)
    for row in range(size):
        for col in range(row, size):
            packed = jnp.where((rows == row) & (cols == col), upper[row][col], packed)
    upper_ref[...] = packed[: upper_ref.shape[0], : upper_ref.shape[1]]
    scale_ref[...] = scale[:1, :1]
    lanes = basis_refs[0].shape[-1] // tile[1]
    weight = [
        [jnp.tile(inverse[j][k] / scale, (1, lanes)) if j <= k else None for k in range(size)]
        for j in range(size)
    ]

    def plane(i, carry):
        parts = [basis_refs[j][i] for j in range(size)]
        for k in range(size):
            acc = parts[0] * weight[0][k]
            for j in range(1, k + 1):
                acc = acc + parts[j] * weight[j][k]
            ortho_ref[k, i] = acc
        return carry

    lax.fori_loop(0, basis_refs[0].shape[0], plane, 0)


def finish(stats, basis, cells):
    size = len(basis)
    vmem = pl.BlockSpec(memory_space=pltpu.VMEM)
    ortho, upper, scale = pl.pallas_call(
        lambda *refs: finish_kernel(float(cells), size, *refs),
        out_shape=(
            jax.ShapeDtypeStruct((size,) + basis[0].shape, jnp.float32),
            jax.ShapeDtypeStruct((size, size), jnp.float32),
            jax.ShapeDtypeStruct((1, 1), jnp.float32),
        ),
        in_specs=[pl.BlockSpec(memory_space=pltpu.SMEM)] + [vmem] * size,
        out_specs=(vmem, vmem, vmem),
    )(stats, *basis)
    return ortho, upper, scale.reshape(())


def wide_exchange(block, depth):
    from_low, from_high = axis_exchange(block[:depth], block[-depth:], "gx")
    block = jnp.concatenate([from_low, block, from_high], axis=0)
    from_low, from_high = axis_exchange(block[:, :depth], block[:, -depth:], "gy")
    return jnp.concatenate([from_low, block, from_high], axis=1)


def shrink_sum(u, coef):
    tx_lo, tx_hi, ty_lo, ty_hi, tz_lo, tz_hi = coef
    centre = u[1:-1, 1:-1]
    zero_plane = jnp.zeros_like(centre[..., :1])
    z_low = jnp.concatenate([zero_plane, centre[..., :-1]], axis=-1)
    z_high = jnp.concatenate([centre[..., 1:], zero_plane], axis=-1)
    total = tx_lo * u[:-2, 1:-1] + tx_hi * u[2:, 1:-1]
    total = total + ty_lo * u[1:-1, :-2] + ty_hi * u[1:-1, 2:]
    total = total + tz_lo * z_low + tz_hi * z_high
    return total


def local(start_field, right_side, accumulation, trans_x, trans_y, trans_z):
    size_x, size_y, size_z = start_field.shape
    cells = size_x * size_y * size_z * lax.axis_size("gx") * lax.axis_size("gy")
    depth = 2

    inputs = (start_field, right_side, accumulation, trans_x, trans_y, trans_z)
    wide = wide_exchange(jnp.concatenate(inputs, axis=-1), depth)
    field, rhs, acc, t_x, t_y, t_z = (wide[..., k * size_z : (k + 1) * size_z] for k in range(len(inputs)))

    first_x = lax.axis_index("gx") * size_x - depth
    first_y = lax.axis_index("gy") * size_y - depth
    grid_x = size_x * lax.axis_size("gx")
    grid_y = size_y * lax.axis_size("gy")

    def region(a, m, dx=0, dy=0):
        o = depth - m
        return a[o + dx : o + dx + size_x + 2 * m, o + dy : o + dy + size_y + 2 * m]

    def inside(m):
        o = depth - m
        gi = first_x + o + lax.broadcasted_iota(jnp.int32, (size_x + 2 * m, 1, 1), 0)
        gj = first_y + o + lax.broadcasted_iota(jnp.int32, (1, size_y + 2 * m, 1), 1)
        return (gi >= 0) & (gi < grid_x) & (gj >= 0) & (gj < grid_y)

    def coefficients(m):
        tz_lo = region(t_z, m)
        return (region(t_x, m), region(t_x, m, 1), region(t_y, m), region(t_y, m, 0, 1), tz_lo, shift_z(tz_lo))

    ring, centre = coefficients(1), coefficients(0)
    tx_lo, tx_hi, ty_lo, ty_hi, tz_lo, tz_hi = ring
    diag_ring = region(acc, 1) + tx_lo + tx_hi + ty_lo + ty_hi + tz_lo + tz_hi
    diag = diag_ring[1:-1, 1:-1]

    residual0 = region(rhs, 1) - (diag_ring * region(field, 1) - shrink_sum(field, ring))
    residual0 = jnp.where(inside(1), residual0, 0.0)

    basis = [residual0[1:-1, 1:-1]]
    basis.append(2.0 * shrink_sum(residual0, centre) / diag)
    vector = jnp.where(inside(1), 2.0 * shrink_sum(wide_exchange(basis[1], depth), ring) / diag_ring, 0.0)
    basis.append(vector[1:-1, 1:-1])
    basis.append(2.0 * shrink_sum(vector, centre) / diag)
    basis.append(2.0 * neighbour_sum(basis[3], field_halo(basis[3]), centre) / diag)
    assert len(basis) == STEPS + 1
    stats = gram(basis)
    stats = all_sum(stats)
    ortho, upper, scale = finish(stats, basis, cells)
    return (ortho, upper, scale)


def solution(mesh):
    in_specs = (
        P("gx", "gy", None),
        P("gx", "gy", None),
        P("gx", "gy", None),
        P("gx", "gy", None),
        P("gx", "gy", None),
        P("gx", "gy", None),
    )
    out_specs = (P(None, "gx", "gy", None), P(), P())
    return jax.shard_map(local, mesh=mesh, in_specs=in_specs, out_specs=out_specs, check_vma=False)
```

```python
import jax
import jax.numpy as jnp
from jax import lax
from jax.sharding import PartitionSpec as P
from jax.experimental import pallas as pl
from jax.experimental.pallas import tpu as pltpu

STEPS = 4


EPS = 1e-06


def shift_pairs(axis, by):
    peers = lax.axis_size(axis)
    return [(i, i + by) for i in range(peers) if 0 <= i + by < peers]


def swap_pairs(axis, parity):
    peers = lax.axis_size(axis)
    pairs = []
    for i in range(parity, peers - 1, 2):
        pairs += [(i, i + 1), (i + 1, i)]
    return pairs


def axis_exchange(to_low, to_high, axis):
    odd = lax.axis_index(axis) % 2 == 1
    even_swap = lax.ppermute(jnp.where(odd, to_low, to_high), axis, swap_pairs(axis, 0))
    odd_swap = lax.ppermute(jnp.where(odd, to_high, to_low), axis, swap_pairs(axis, 1))
    from_low = jnp.where(odd, even_swap, odd_swap)
    from_high = jnp.where(odd, odd_swap, even_swap)
    return from_low, from_high


def exchange(to_low_x, to_high_x, to_low_y, to_high_y):
    from_low_x, from_high_x = axis_exchange(to_low_x, to_high_x, "gx")
    from_low_y, from_high_y = axis_exchange(to_low_y, to_high_y, "gy")
    return from_low_x, from_high_x, from_low_y, from_high_y


def neighbour_sum(u, halo, coef):
    lo_x, hi_x, lo_y, hi_y = halo
    tx_lo, tx_hi, ty_lo, ty_hi, tz_lo, tz_hi = coef
    zero_plane = jnp.zeros_like(u[..., :1])
    u_xm = jnp.concatenate([lo_x, u[:-1]], axis=0)
    u_xp = jnp.concatenate([u[1:], hi_x], axis=0)
    u_ym = jnp.concatenate([lo_y, u[:, :-1]], axis=1)
    u_yp = jnp.concatenate([u[:, 1:], hi_y], axis=1)
    u_zm = jnp.concatenate([zero_plane, u[..., :-1]], axis=-1)
    u_zp = jnp.concatenate([u[..., 1:], zero_plane], axis=-1)
    total = tx_lo * u_xm + tx_hi * u_xp
    total = total + ty_lo * u_ym + ty_hi * u_yp
    total = total + tz_lo * u_zm + tz_hi * u_zp
    return total


def field_halo(u):
    return exchange(u[:1], u[-1:], u[:, :1], u[:, -1:])


def shift_z(a):
    return jnp.concatenate([a[..., 1:], jnp.zeros_like(a[..., :1])], axis=-1)


def all_sum(x):
    for axis in ("gy", "gx"):
        n = lax.axis_size(axis)
        if n & (n - 1):
            x = lax.psum(x, axis)
            continue
        step = 1
        while step < n:
            x = x + lax.ppermute(x, axis, [(i, i ^ step) for i in range(n)])
            step *= 2
    return x


def gram_kernel(size, *refs):
    basis_refs, out_ref = refs[:size], refs[size]
    tile = out_ref.shape
    pairs = [(a, b) for a in range(size) for b in range(a, size)]
    planes, rows, lanes = basis_refs[0].shape
    chunks = lanes // tile[1]

    def plane(i, accs):
        accs = list(accs)
        for c in range(chunks):
            parts = [r[i, :, c * tile[1] : (c + 1) * tile[1]] for r in basis_refs]
            for n, (a, b) in enumerate(pairs):
                accs[n] = accs[n] + parts[a] * parts[b]
        return tuple(accs)

    zero = jnp.zeros((rows, tile[1]), jnp.float32)
    accs = lax.fori_loop(0, planes, plane, tuple(zero for _ in pairs))
    row_ids = lax.broadcasted_iota(jnp.int32, tile, 0)
    lane_ids = lax.broadcasted_iota(jnp.int32, tile, 1)
    packed = jnp.zeros(tile, jnp.float32)
    for n, (a, b) in enumerate(pairs):
        total = jnp.sum(accs[n])
        hit = (lane_ids == 1 + a * size + b) | (lane_ids == 1 + b * size + a)
        if a == 0 and b == 0:
            hit = hit | (lane_ids == 0)
        packed = jnp.where((row_ids == 0) & hit, total, packed)
    out_ref[...] = packed


def gram(basis):
    size = len(basis)
    vmem = pl.BlockSpec(memory_space=pltpu.VMEM)
    return pl.pallas_call(
        lambda *refs: gram_kernel(size, *refs),
        out_shape=jax.ShapeDtypeStruct((8, 128), jnp.float32),
        in_specs=[vmem] * size,
        out_specs=vmem,
    )(*basis)


def finish_kernel(cells, size, stats_ref, *refs):
    basis_refs, (ortho_ref, upper_ref, scale_ref) = refs[:size], refs[size:]
    tile = (8, 128)

    def held(i):
        return jnp.full(tile, stats_ref[0, i], jnp.float32)

    scale = jnp.sqrt(held(0) / cells + EPS)
    square = scale * scale
    gram = [[held(1 + a * size + b) / cells / square for b in range(size)] for a in range(size)]
    upper = [[None] * size for _ in range(size)]
    for row in range(size):
        value = gram[row][row]
        for prev in range(row):
            value = value - upper[prev][row] * upper[prev][row]
        pivot = jnp.sqrt(value)
        upper[row][row] = pivot
        for col in range(row + 1, size):
            value = gram[row][col]
            for prev in range(row):
                value = value - upper[prev][row] * upper[prev][col]
            upper[row][col] = value / pivot
    inverse = [[None] * size for _ in range(size)]
    for col in range(size):
        for row in reversed(range(col + 1)):
            value = jnp.full(tile, 1.0 if row == col else 0.0, jnp.float32)
            for inner in range(row + 1, col + 1):
                value = value - upper[row][inner] * inverse[inner][col]
            inverse[row][col] = value / upper[row][row]
    rows = lax.broadcasted_iota(jnp.int32, tile, 0)
    cols = lax.broadcasted_iota(jnp.int32, tile, 1)
    packed = jnp.zeros(tile, jnp.float32)
    for row in range(size):
        for col in range(row, size):
            packed = jnp.where((rows == row) & (cols == col), upper[row][col], packed)
    upper_ref[...] = packed[: upper_ref.shape[0], : upper_ref.shape[1]]
    scale_ref[...] = scale[:1, :1]
    lanes = basis_refs[0].shape[-1] // tile[1]
    weight = [
        [jnp.tile(inverse[j][k] / scale, (1, lanes)) if j <= k else None for k in range(size)]
        for j in range(size)
    ]

    def plane(i, carry):
        parts = [basis_refs[j][i] for j in range(size)]
        for k in range(size):
            acc = parts[0] * weight[0][k]
            for j in range(1, k + 1):
                acc = acc + parts[j] * weight[j][k]
            ortho_ref[k, i] = acc
        return carry

    lax.fori_loop(0, basis_refs[0].shape[0], plane, 0)


def finish(stats, basis, cells):
    size = len(basis)
    vmem = pl.BlockSpec(memory_space=pltpu.VMEM)
    ortho, upper, scale = pl.pallas_call(
        lambda *refs: finish_kernel(float(cells), size, *refs),
        out_shape=(
            jax.ShapeDtypeStruct((size,) + basis[0].shape, jnp.float32),
            jax.ShapeDtypeStruct((size, size), jnp.float32),
            jax.ShapeDtypeStruct((1, 1), jnp.float32),
        ),
        in_specs=[pl.BlockSpec(memory_space=pltpu.SMEM)] + [vmem] * size,
        out_specs=(vmem, vmem, vmem),
    )(stats, *basis)
    return ortho, upper, scale.reshape(())


def wide_exchange(blocks, depth):
    lanes = blocks[0].shape[-1]

    def edges(parts, dim):
        low = jnp.concatenate([lax.slice_in_dim(p, 0, depth, axis=dim) for p in parts], axis=-1)
        high = jnp.concatenate([lax.slice_in_dim(p, p.shape[dim] - depth, None, axis=dim) for p in parts], axis=-1)
        return low, high

    for axis, dim in (("gx", 0), ("gy", 1)):
        from_low, from_high = axis_exchange(*edges(blocks, dim), axis)
        blocks = [
            jnp.concatenate([from_low[..., k * lanes : (k + 1) * lanes], b, from_high[..., k * lanes : (k + 1) * lanes]], axis=dim)
            for k, b in enumerate(blocks)
        ]
    return blocks


def shrink_sum(u, coef):
    tx_lo, tx_hi, ty_lo, ty_hi, tz_lo, tz_hi = coef
    centre = u[1:-1, 1:-1]
    zero_plane = jnp.zeros_like(centre[..., :1])
    z_low = jnp.concatenate([zero_plane, centre[..., :-1]], axis=-1)
    z_high = jnp.concatenate([centre[..., 1:], zero_plane], axis=-1)
    total = tx_lo * u[:-2, 1:-1] + tx_hi * u[2:, 1:-1]
    total = total + ty_lo * u[1:-1, :-2] + ty_hi * u[1:-1, 2:]
    total = total + tz_lo * z_low + tz_hi * z_high
    return total


def local(start_field, right_side, accumulation, trans_x, trans_y, trans_z):
    size_x, size_y, size_z = start_field.shape
    cells = size_x * size_y * size_z * lax.axis_size("gx") * lax.axis_size("gy")
    depth = 2

    inputs = (start_field, right_side, accumulation, trans_x, trans_y, trans_z)
    field, rhs, acc, t_x, t_y, t_z = wide_exchange(inputs, depth)

    first_x = lax.axis_index("gx") * size_x - depth
    first_y = lax.axis_index("gy") * size_y - depth
    grid_x = size_x * lax.axis_size("gx")
    grid_y = size_y * lax.axis_size("gy")

    def region(a, m, dx=0, dy=0):
        o = depth - m
        return a[o + dx : o + dx + size_x + 2 * m, o + dy : o + dy + size_y + 2 * m]

    def inside(m):
        o = depth - m
        gi = first_x + o + lax.broadcasted_iota(jnp.int32, (size_x + 2 * m, 1, 1), 0)
        gj = first_y + o + lax.broadcasted_iota(jnp.int32, (1, size_y + 2 * m, 1), 1)
        return (gi >= 0) & (gi < grid_x) & (gj >= 0) & (gj < grid_y)

    def coefficients(m):
        tz_lo = region(t_z, m)
        return (region(t_x, m), region(t_x, m, 1), region(t_y, m), region(t_y, m, 0, 1), tz_lo, shift_z(tz_lo))

    ring, centre = coefficients(1), coefficients(0)
    tx_lo, tx_hi, ty_lo, ty_hi, tz_lo, tz_hi = ring
    diag_ring = region(acc, 1) + tx_lo + tx_hi + ty_lo + ty_hi + tz_lo + tz_hi
    diag = diag_ring[1:-1, 1:-1]

    residual0 = region(rhs, 1) - (diag_ring * region(field, 1) - shrink_sum(field, ring))
    residual0 = jnp.where(inside(1), residual0, 0.0)

    basis = [residual0[1:-1, 1:-1]]
    basis.append(2.0 * shrink_sum(residual0, centre) / diag)
    vector = jnp.where(inside(1), 2.0 * shrink_sum(wide_exchange([basis[1]], depth)[0], ring) / diag_ring, 0.0)
    basis.append(vector[1:-1, 1:-1])
    basis.append(2.0 * shrink_sum(vector, centre) / diag)
    basis.append(2.0 * neighbour_sum(basis[3], field_halo(basis[3]), centre) / diag)
    assert len(basis) == STEPS + 1
    stats = gram(basis)
    stats = all_sum(stats)
    ortho, upper, scale = finish(stats, basis, cells)
    return (ortho, upper, scale)


def solution(mesh):
    in_specs = (
        P("gx", "gy", None),
        P("gx", "gy", None),
        P("gx", "gy", None),
        P("gx", "gy", None),
        P("gx", "gy", None),
        P("gx", "gy", None),
    )
    out_specs = (P(None, "gx", "gy", None), P(), P())
    return jax.shard_map(local, mesh=mesh, in_specs=in_specs, out_specs=out_specs, check_vma=False)
```

```python
import jax
import jax.numpy as jnp
from jax import lax
from jax.sharding import PartitionSpec as P
from jax.experimental import pallas as pl
from jax.experimental.pallas import tpu as pltpu

STEPS = 4


EPS = 1e-06


def shift_pairs(axis, by):
    peers = lax.axis_size(axis)
    return [(i, i + by) for i in range(peers) if 0 <= i + by < peers]


def swap_pairs(axis, parity):
    peers = lax.axis_size(axis)
    pairs = []
    for i in range(parity, peers - 1, 2):
        pairs += [(i, i + 1), (i + 1, i)]
    return pairs


def axis_exchange(to_low, to_high, axis):
    odd = lax.axis_index(axis) % 2 == 1
    even_swap = lax.ppermute(jnp.where(odd, to_low, to_high), axis, swap_pairs(axis, 0))
    odd_swap = lax.ppermute(jnp.where(odd, to_high, to_low), axis, swap_pairs(axis, 1))
    from_low = jnp.where(odd, even_swap, odd_swap)
    from_high = jnp.where(odd, odd_swap, even_swap)
    return from_low, from_high


def exchange(to_low_x, to_high_x, to_low_y, to_high_y):
    from_low_x, from_high_x = axis_exchange(to_low_x, to_high_x, "gx")
    from_low_y, from_high_y = axis_exchange(to_low_y, to_high_y, "gy")
    return from_low_x, from_high_x, from_low_y, from_high_y


def neighbour_sum(u, halo, coef, rows=None, cols=None):
    lo_x, hi_x, lo_y, hi_y = halo
    r0, r1 = rows or (0, u.shape[0])
    c0, c1 = cols or (0, u.shape[1])
    tx_lo, tx_hi, ty_lo, ty_hi, tz_lo, tz_hi = (c[r0:r1, c0:c1] for c in coef)
    along_x = jnp.concatenate([lo_x, u, hi_x], axis=0)[:, c0:c1]
    along_y = jnp.concatenate([lo_y, u, hi_y], axis=1)[r0:r1]
    centre = u[r0:r1, c0:c1]
    zero_plane = jnp.zeros_like(centre[..., :1])
    u_zm = jnp.concatenate([zero_plane, centre[..., :-1]], axis=-1)
    u_zp = jnp.concatenate([centre[..., 1:], zero_plane], axis=-1)
    total = tx_lo * along_x[r0:r1] + tx_hi * along_x[r0 + 2 : r1 + 2]
    total = total + ty_lo * along_y[:, c0:c1] + ty_hi * along_y[:, c0 + 2 : c1 + 2]
    total = total + tz_lo * u_zm + tz_hi * u_zp
    return total


def faces(u):
    return u[:1], u[-1:], u[:, :1], u[:, -1:]


def field_halo(u):
    return exchange(*faces(u))


def all_sum(x):
    for axis in ("gy", "gx"):
        n = lax.axis_size(axis)
        if n & (n - 1):
            x = lax.psum(x, axis)
            continue
        step = 1
        while step < n:
            x = x + lax.ppermute(x, axis, [(i, i ^ step) for i in range(n)])
            step *= 2
    return x


def gram_kernel(size, *refs):
    basis_refs, out_ref = refs[:size], refs[size]
    tile = out_ref.shape
    pairs = [(a, b) for a in range(size) for b in range(a, size)]
    planes, rows, lanes = basis_refs[0].shape
    chunks = lanes // tile[1]

    def plane(i, accs):
        accs = list(accs)
        for c in range(chunks):
            parts = [r[i, :, c * tile[1] : (c + 1) * tile[1]] for r in basis_refs]
            for n, (a, b) in enumerate(pairs):
                accs[n] = accs[n] + parts[a] * parts[b]
        return tuple(accs)

    zero = jnp.zeros((rows, tile[1]), jnp.float32)
    accs = lax.fori_loop(0, planes, plane, tuple(zero for _ in pairs))
    row_ids = lax.broadcasted_iota(jnp.int32, tile, 0)
    lane_ids = lax.broadcasted_iota(jnp.int32, tile, 1)
    packed = jnp.zeros(tile, jnp.float32)
    for n, (a, b) in enumerate(pairs):
        total = jnp.sum(accs[n])
        hit = (lane_ids == 1 + a * size + b) | (lane_ids == 1 + b * size + a)
        if a == 0 and b == 0:
            hit = hit | (lane_ids == 0)
        packed = jnp.where((row_ids == 0) & hit, total, packed)
    out_ref[...] = packed


def gram(basis):
    size = len(basis)
    vmem = pl.BlockSpec(memory_space=pltpu.VMEM)
    return pl.pallas_call(
        lambda *refs: gram_kernel(size, *refs),
        out_shape=jax.ShapeDtypeStruct((8, 128), jnp.float32),
        in_specs=[vmem] * size,
        out_specs=vmem,
    )(*basis)


def finish_kernel(cells, size, stats_ref, *refs):
    basis_refs, (ortho_ref, upper_ref, scale_ref) = refs[:size], refs[size:]
    tile = (8, 128)

    def held(i):
        return jnp.full(tile, stats_ref[0, i], jnp.float32)

    scale = jnp.sqrt(held(0) / cells + EPS)
    square = scale * scale
    gram = [[held(1 + a * size + b) / cells / square for b in range(size)] for a in range(size)]
    upper = [[None] * size for _ in range(size)]
    for row in range(size):
        value = gram[row][row]
        for prev in range(row):
            value = value - upper[prev][row] * upper[prev][row]
        pivot = jnp.sqrt(value)
        upper[row][row] = pivot
        for col in range(row + 1, size):
            value = gram[row][col]
            for prev in range(row):
                value = value - upper[prev][row] * upper[prev][col]
            upper[row][col] = value / pivot
    inverse = [[None] * size for _ in range(size)]
    for col in range(size):
        for row in reversed(range(col + 1)):
            value = jnp.full(tile, 1.0 if row == col else 0.0, jnp.float32)
            for inner in range(row + 1, col + 1):
                value = value - upper[row][inner] * inverse[inner][col]
            inverse[row][col] = value / upper[row][row]
    rows = lax.broadcasted_iota(jnp.int32, tile, 0)
    cols = lax.broadcasted_iota(jnp.int32, tile, 1)
    packed = jnp.zeros(tile, jnp.float32)
    for row in range(size):
        for col in range(row, size):
            packed = jnp.where((rows == row) & (cols == col), upper[row][col], packed)
    upper_ref[...] = packed[: upper_ref.shape[0], : upper_ref.shape[1]]
    scale_ref[...] = scale[:1, :1]
    lanes = basis_refs[0].shape[-1] // tile[1]
    weight = [
        [jnp.tile(inverse[j][k] / scale, (1, lanes)) if j <= k else None for k in range(size)]
        for j in range(size)
    ]

    def plane(i, carry):
        parts = [basis_refs[j][i] for j in range(size)]
        for k in range(size):
            acc = parts[0] * weight[0][k]
            for j in range(1, k + 1):
                acc = acc + parts[j] * weight[j][k]
            ortho_ref[k, i] = acc
        return carry

    lax.fori_loop(0, basis_refs[0].shape[0], plane, 0)


def finish(stats, basis, cells):
    size = len(basis)
    vmem = pl.BlockSpec(memory_space=pltpu.VMEM)
    ortho, upper, scale = pl.pallas_call(
        lambda *refs: finish_kernel(float(cells), size, *refs),
        out_shape=(
            jax.ShapeDtypeStruct((size,) + basis[0].shape, jnp.float32),
            jax.ShapeDtypeStruct((size, size), jnp.float32),
            jax.ShapeDtypeStruct((1, 1), jnp.float32),
        ),
        in_specs=[pl.BlockSpec(memory_space=pltpu.SMEM)] + [vmem] * size,
        out_specs=(vmem, vmem, vmem),
    )(stats, *basis)
    return ortho, upper, scale.reshape(())


def local(start_field, right_side, accumulation, trans_x, trans_y, trans_z):
    size_x, size_y, size_z = start_field.shape
    cells = size_x * size_y * size_z * lax.axis_size("gx") * lax.axis_size("gy")

    lo_both_x, hi_both_x, lo_both_y, hi_both_y = exchange(
        jnp.concatenate([start_field[:1], trans_x[:1]], axis=0),
        jnp.concatenate([start_field[-1:], trans_x[-1:]], axis=0),
        jnp.concatenate([start_field[:, :1], trans_y[:, :1]], axis=1),
        jnp.concatenate([start_field[:, -1:], trans_y[:, -1:]], axis=1),
    )
    lo_x, hi_x, plane_x = lo_both_x[:1], hi_both_x[:1], hi_both_x[1:]
    lo_y, hi_y, plane_y = lo_both_y[:, :1], hi_both_y[:, :1], hi_both_y[:, 1:]

    zero_plane = jnp.zeros_like(trans_z[..., :1])
    tx_lo = trans_x
    tx_hi = jnp.concatenate([trans_x[1:], plane_x], axis=0)
    ty_lo = trans_y
    ty_hi = jnp.concatenate([trans_y[:, 1:], plane_y], axis=1)
    tz_lo = trans_z
    tz_hi = jnp.concatenate([trans_z[..., 1:], zero_plane], axis=-1)
    coef = (tx_lo, tx_hi, ty_lo, ty_hi, tz_lo, tz_hi)
    diagonal = accumulation + tx_lo + tx_hi + ty_lo + ty_hi + tz_lo + tz_hi

    halo = (lo_x, hi_x, lo_y, hi_y)
    size_x, size_y = start_field.shape[:2]
    face_regions = (((0, 1), None), ((size_x - 1, size_x), None), (None, (0, 1)), (None, (size_y - 1, size_y)))

    def residual(rows=None, cols=None):
        part = lambda a: a[slice(*(rows or (0, size_x))), slice(*(cols or (0, size_y)))]
        total = neighbour_sum(start_field, halo, coef, rows, cols)
        return part(right_side) - (part(diagonal) * part(start_field) - total)

    def step(u, u_halo, rows=None, cols=None):
        part = diagonal[slice(*(rows or (0, size_x))), slice(*(cols or (0, size_y)))]
        return 2.0 * neighbour_sum(u, u_halo, coef, rows, cols) / part

    next_halo = exchange(*(residual(r, c) for r, c in face_regions))
    vector = residual()
    basis = [vector]
    for step_index in range(STEPS):
        halo = next_halo
        if step_index < STEPS - 1:
            next_halo = exchange(*(step(vector, halo, r, c) for r, c in face_regions))
        vector = step(vector, halo)
        basis.append(vector)
    stats = gram(basis)
    stats = all_sum(stats)
    ortho, upper, scale = finish(stats, basis, cells)
    return (ortho, upper, scale)


def solution(mesh):
    in_specs = (
        P("gx", "gy", None),
        P("gx", "gy", None),
        P("gx", "gy", None),
        P("gx", "gy", None),
        P("gx", "gy", None),
        P("gx", "gy", None),
    )
    out_specs = (P(None, "gx", "gy", None), P(), P())
    return jax.shard_map(local, mesh=mesh, in_specs=in_specs, out_specs=out_specs, check_vma=False)
```

```python
import jax
import jax.numpy as jnp
from jax import lax
from jax.sharding import PartitionSpec as P
from jax.experimental import pallas as pl
from jax.experimental.pallas import tpu as pltpu

STEPS = 4


EPS = 1e-06


def shift_pairs(axis, by):
    peers = lax.axis_size(axis)
    return [(i, i + by) for i in range(peers) if 0 <= i + by < peers]


def swap_pairs(axis, parity):
    peers = lax.axis_size(axis)
    pairs = []
    for i in range(parity, peers - 1, 2):
        pairs += [(i, i + 1), (i + 1, i)]
    return pairs


def axis_exchange(to_low, to_high, axis):
    odd = lax.axis_index(axis) % 2 == 1
    even_swap = lax.ppermute(jnp.where(odd, to_low, to_high), axis, swap_pairs(axis, 0))
    odd_swap = lax.ppermute(jnp.where(odd, to_high, to_low), axis, swap_pairs(axis, 1))
    from_low = jnp.where(odd, even_swap, odd_swap)
    from_high = jnp.where(odd, odd_swap, even_swap)
    return from_low, from_high


def exchange(to_low_x, to_high_x, to_low_y, to_high_y):
    from_low_x, from_high_x = axis_exchange(to_low_x, to_high_x, "gx")
    from_low_y, from_high_y = axis_exchange(to_low_y, to_high_y, "gy")
    return from_low_x, from_high_x, from_low_y, from_high_y


def neighbour_sum(u, halo, coef):
    lo_x, hi_x, lo_y, hi_y = halo
    tx_lo, tx_hi, ty_lo, ty_hi, tz_lo, tz_hi = coef
    zero_plane = jnp.zeros_like(u[..., :1])
    u_xm = jnp.concatenate([lo_x, u[:-1]], axis=0)
    u_xp = jnp.concatenate([u[1:], hi_x], axis=0)
    u_ym = jnp.concatenate([lo_y, u[:, :-1]], axis=1)
    u_yp = jnp.concatenate([u[:, 1:], hi_y], axis=1)
    u_zm = jnp.concatenate([zero_plane, u[..., :-1]], axis=-1)
    u_zp = jnp.concatenate([u[..., 1:], zero_plane], axis=-1)
    total = tx_lo * u_xm + tx_hi * u_xp
    total = total + ty_lo * u_ym + ty_hi * u_yp
    total = total + tz_lo * u_zm + tz_hi * u_zp
    return total


def field_halo(u):
    return exchange(u[:1], u[-1:], u[:, :1], u[:, -1:])


def all_sum(x):
    for axis in ("gy", "gx"):
        n = lax.axis_size(axis)
        if n & (n - 1):
            x = lax.psum(x, axis)
            continue
        step = 1
        while step < n:
            x = x + lax.ppermute(x, axis, [(i, i ^ step) for i in range(n)])
            step *= 2
    return x


def gram_kernel(size, pairs, count, *refs):
    basis_refs, rest = refs[:count], refs[count:]
    out_ref = rest[-1]
    tile = out_ref.shape
    planes, rows, lanes = basis_refs[0].shape
    chunks = lanes // tile[1]

    def plane(i, accs):
        accs = list(accs)
        for c in range(chunks):
            parts = [r[i, :, c * tile[1] : (c + 1) * tile[1]] for r in basis_refs]
            for n, (a, b) in enumerate(pairs):
                accs[n] = accs[n] + parts[a] * parts[b]
        return tuple(accs)

    zero = jnp.zeros((rows, tile[1]), jnp.float32)
    accs = lax.fori_loop(0, planes, plane, tuple(zero for _ in pairs))
    row_ids = lax.broadcasted_iota(jnp.int32, tile, 0)
    lane_ids = lax.broadcasted_iota(jnp.int32, tile, 1)
    packed = rest[0][...] if len(rest) > 1 else jnp.zeros(tile, jnp.float32)
    for n, (a, b) in enumerate(pairs):
        total = jnp.sum(accs[n])
        hit = (lane_ids == 1 + a * size + b) | (lane_ids == 1 + b * size + a)
        if a == 0 and b == 0:
            hit = hit | (lane_ids == 0)
        packed = jnp.where((row_ids == 0) & hit, total, packed)
    out_ref[...] = packed


def gram(vectors, pairs, size, base=None):
    vmem = pl.BlockSpec(memory_space=pltpu.VMEM)
    extra = [] if base is None else [base]
    return pl.pallas_call(
        lambda *refs: gram_kernel(size, pairs, len(vectors), *refs),
        out_shape=jax.ShapeDtypeStruct((8, 128), jnp.float32),
        in_specs=[vmem] * (len(vectors) + len(extra)),
        out_specs=vmem,
    )(*vectors, *extra)


def finish_kernel(cells, size, stats_ref, *refs):
    basis_refs, (ortho_ref, upper_ref, scale_ref) = refs[:size], refs[size:]
    tile = (8, 128)

    def held(i):
        return jnp.full(tile, stats_ref[0, i], jnp.float32)

    scale = jnp.sqrt(held(0) / cells + EPS)
    square = scale * scale
    gram = [[held(1 + a * size + b) / cells / square for b in range(size)] for a in range(size)]
    upper = [[None] * size for _ in range(size)]
    for row in range(size):
        value = gram[row][row]
        for prev in range(row):
            value = value - upper[prev][row] * upper[prev][row]
        pivot = jnp.sqrt(value)
        upper[row][row] = pivot
        for col in range(row + 1, size):
            value = gram[row][col]
            for prev in range(row):
                value = value - upper[prev][row] * upper[prev][col]
            upper[row][col] = value / pivot
    inverse = [[None] * size for _ in range(size)]
    for col in range(size):
        for row in reversed(range(col + 1)):
            value = jnp.full(tile, 1.0 if row == col else 0.0, jnp.float32)
            for inner in range(row + 1, col + 1):
                value = value - upper[row][inner] * inverse[inner][col]
            inverse[row][col] = value / upper[row][row]
    rows = lax.broadcasted_iota(jnp.int32, tile, 0)
    cols = lax.broadcasted_iota(jnp.int32, tile, 1)
    packed = jnp.zeros(tile, jnp.float32)
    for row in range(size):
        for col in range(row, size):
            packed = jnp.where((rows == row) & (cols == col), upper[row][col], packed)
    upper_ref[...] = packed[: upper_ref.shape[0], : upper_ref.shape[1]]
    scale_ref[...] = scale[:1, :1]
    lanes = basis_refs[0].shape[-1] // tile[1]
    weight = [
        [jnp.tile(inverse[j][k] / scale, (1, lanes)) if j <= k else None for k in range(size)]
        for j in range(size)
    ]

    def plane(i, carry):
        parts = [basis_refs[j][i] for j in range(size)]
        for k in range(size):
            acc = parts[0] * weight[0][k]
            for j in range(1, k + 1):
                acc = acc + parts[j] * weight[j][k]
            ortho_ref[k, i] = acc
        return carry

    lax.fori_loop(0, basis_refs[0].shape[0], plane, 0)


def finish(stats, basis, cells):
    size = len(basis)
    vmem = pl.BlockSpec(memory_space=pltpu.VMEM)
    ortho, upper, scale = pl.pallas_call(
        lambda *refs: finish_kernel(float(cells), size, *refs),
        out_shape=(
            jax.ShapeDtypeStruct((size,) + basis[0].shape, jnp.float32),
            jax.ShapeDtypeStruct((size, size), jnp.float32),
            jax.ShapeDtypeStruct((1, 1), jnp.float32),
        ),
        in_specs=[pl.BlockSpec(memory_space=pltpu.SMEM)] + [vmem] * size,
        out_specs=(vmem, vmem, vmem),
    )(stats, *basis)
    return ortho, upper, scale.reshape(())


def local(start_field, right_side, accumulation, trans_x, trans_y, trans_z):
    size_x, size_y, size_z = start_field.shape
    cells = size_x * size_y * size_z * lax.axis_size("gx") * lax.axis_size("gy")

    lo_both_x, hi_both_x, lo_both_y, hi_both_y = exchange(
        jnp.concatenate([start_field[:1], trans_x[:1]], axis=0),
        jnp.concatenate([start_field[-1:], trans_x[-1:]], axis=0),
        jnp.concatenate([start_field[:, :1], trans_y[:, :1]], axis=1),
        jnp.concatenate([start_field[:, -1:], trans_y[:, -1:]], axis=1),
    )
    lo_x, hi_x, plane_x = lo_both_x[:1], hi_both_x[:1], hi_both_x[1:]
    lo_y, hi_y, plane_y = lo_both_y[:, :1], hi_both_y[:, :1], hi_both_y[:, 1:]

    zero_plane = jnp.zeros_like(trans_z[..., :1])
    tx_lo = trans_x
    tx_hi = jnp.concatenate([trans_x[1:], plane_x], axis=0)
    ty_lo = trans_y
    ty_hi = jnp.concatenate([trans_y[:, 1:], plane_y], axis=1)
    tz_lo = trans_z
    tz_hi = jnp.concatenate([trans_z[..., 1:], zero_plane], axis=-1)
    coef = (tx_lo, tx_hi, ty_lo, ty_hi, tz_lo, tz_hi)
    diagonal = accumulation + tx_lo + tx_hi + ty_lo + ty_hi + tz_lo + tz_hi

    total = neighbour_sum(start_field, (lo_x, hi_x, lo_y, hi_y), coef)
    residual0 = right_side - (diagonal * start_field - total)

    vector = residual0
    basis = [vector]
    for step in range(STEPS):
        if step == STEPS - 1:
            early = [(a, b) for a in range(STEPS) for b in range(a, STEPS)]
            stats = gram(basis, early, STEPS + 1)
        total = neighbour_sum(vector, field_halo(vector), coef)
        vector = 2.0 * total / diagonal
        basis.append(vector)
    stats = gram(basis, [(a, STEPS) for a in range(STEPS + 1)], STEPS + 1, stats)
    stats = all_sum(stats)
    ortho, upper, scale = finish(stats, basis, cells)
    return (ortho, upper, scale)


def solution(mesh):
    in_specs = (
        P("gx", "gy", None),
        P("gx", "gy", None),
        P("gx", "gy", None),
        P("gx", "gy", None),
        P("gx", "gy", None),
        P("gx", "gy", None),
    )
    out_specs = (P(None, "gx", "gy", None), P(), P())
    return jax.shard_map(local, mesh=mesh, in_specs=in_specs, out_specs=out_specs, check_vma=False)
```

```python
import jax
import jax.numpy as jnp
from jax import lax
from jax.sharding import PartitionSpec as P
from jax.experimental import pallas as pl
from jax.experimental.pallas import tpu as pltpu

STEPS = 4


EPS = 1e-06


def shift_pairs(axis, by):
    peers = lax.axis_size(axis)
    return [(i, i + by) for i in range(peers) if 0 <= i + by < peers]


def swap_pairs(axis, parity):
    peers = lax.axis_size(axis)
    pairs = []
    for i in range(parity, peers - 1, 2):
        pairs += [(i, i + 1), (i + 1, i)]
    return pairs


def axis_exchange(to_low, to_high, axis):
    odd = lax.axis_index(axis) % 2 == 1
    even_swap = lax.ppermute(jnp.where(odd, to_low, to_high), axis, swap_pairs(axis, 0))
    odd_swap = lax.ppermute(jnp.where(odd, to_high, to_low), axis, swap_pairs(axis, 1))
    from_low = jnp.where(odd, even_swap, odd_swap)
    from_high = jnp.where(odd, odd_swap, even_swap)
    return from_low, from_high


def exchange(to_low_x, to_high_x, to_low_y, to_high_y):
    from_low_x, from_high_x = axis_exchange(to_low_x, to_high_x, "gx")
    from_low_y, from_high_y = axis_exchange(to_low_y, to_high_y, "gy")
    return from_low_x, from_high_x, from_low_y, from_high_y


def neighbour_sum(u, halo, coef):
    lo_x, hi_x, lo_y, hi_y = halo
    tx_lo, tx_hi, ty_lo, ty_hi, tz_lo, tz_hi = coef
    zero_plane = jnp.zeros_like(u[..., :1])
    u_xm = jnp.concatenate([lo_x, u[:-1]], axis=0)
    u_xp = jnp.concatenate([u[1:], hi_x], axis=0)
    u_ym = jnp.concatenate([lo_y, u[:, :-1]], axis=1)
    u_yp = jnp.concatenate([u[:, 1:], hi_y], axis=1)
    u_zm = jnp.concatenate([zero_plane, u[..., :-1]], axis=-1)
    u_zp = jnp.concatenate([u[..., 1:], zero_plane], axis=-1)
    total = tx_lo * u_xm + tx_hi * u_xp
    total = total + ty_lo * u_ym + ty_hi * u_yp
    total = total + tz_lo * u_zm + tz_hi * u_zp
    return total


def field_halo(u):
    return exchange(u[:1], u[-1:], u[:, :1], u[:, -1:])


def all_sum(x):
    for axis in ("gy", "gx"):
        n = lax.axis_size(axis)
        if n & (n - 1):
            x = lax.psum(x, axis)
            continue
        step = 1
        while step < n:
            x = x + lax.ppermute(x, axis, [(i, i ^ step) for i in range(n)])
            step *= 2
    return x


def gram_kernel(size, *refs):
    basis_refs, out_ref = refs[:size], refs[size]
    tile = out_ref.shape
    pairs = [(a, b) for a in range(size) for b in range(a, size)]
    planes, rows, lanes = basis_refs[0].shape
    chunks = lanes // tile[1]

    def plane(i, accs):
        accs = list(accs)
        for c in range(chunks):
            parts = [r[i, :, c * tile[1] : (c + 1) * tile[1]] for r in basis_refs]
            for n, (a, b) in enumerate(pairs):
                accs[n] = accs[n] + parts[a] * parts[b]
        return tuple(accs)

    zero = jnp.zeros((rows, tile[1]), jnp.float32)
    accs = lax.fori_loop(0, planes, plane, tuple(zero for _ in pairs))
    row_ids = lax.broadcasted_iota(jnp.int32, tile, 0)
    lane_ids = lax.broadcasted_iota(jnp.int32, tile, 1)
    packed = jnp.zeros(tile, jnp.float32)
    for n, (a, b) in enumerate(pairs):
        total = jnp.sum(accs[n])
        hit = (lane_ids == 1 + a * size + b) | (lane_ids == 1 + b * size + a)
        if a == 0 and b == 0:
            hit = hit | (lane_ids == 0)
        packed = jnp.where((row_ids == 0) & hit, total, packed)
    out_ref[...] = packed


def gram(basis):
    size = len(basis)
    vmem = pl.BlockSpec(memory_space=pltpu.VMEM)
    return pl.pallas_call(
        lambda *refs: gram_kernel(size, *refs),
        out_shape=jax.ShapeDtypeStruct((8, 128), jnp.float32),
        in_specs=[vmem] * size,
        out_specs=vmem,
    )(*basis)


def finish_kernel(cells, size, stats_ref, *refs):
    basis_refs, (ortho_ref, upper_ref, scale_ref) = refs[:size], refs[size:]
    tile = (8, 128)

    def held(i):
        return jnp.full(tile, stats_ref[0, i], jnp.float32)

    scale = jnp.sqrt(held(0) / cells + EPS)
    square = scale * scale
    gram = [[held(1 + a * size + b) / cells / square for b in range(size)] for a in range(size)]
    upper = [[None] * size for _ in range(size)]
    for row in range(size):
        value = gram[row][row]
        for prev in range(row):
            value = value - upper[prev][row] * upper[prev][row]
        pivot = jnp.sqrt(value)
        upper[row][row] = pivot
        for col in range(row + 1, size):
            value = gram[row][col]
            for prev in range(row):
                value = value - upper[prev][row] * upper[prev][col]
            upper[row][col] = value / pivot
    inverse = [[None] * size for _ in range(size)]
    for col in range(size):
        for row in reversed(range(col + 1)):
            value = jnp.full(tile, 1.0 if row == col else 0.0, jnp.float32)
            for inner in range(row + 1, col + 1):
                value = value - upper[row][inner] * inverse[inner][col]
            inverse[row][col] = value / upper[row][row]
    rows = lax.broadcasted_iota(jnp.int32, tile, 0)
    cols = lax.broadcasted_iota(jnp.int32, tile, 1)
    packed = jnp.zeros(tile, jnp.float32)
    for row in range(size):
        for col in range(row, size):
            packed = jnp.where((rows == row) & (cols == col), upper[row][col], packed)
    upper_ref[...] = packed[: upper_ref.shape[0], : upper_ref.shape[1]]
    scale_ref[...] = scale[:1, :1]
    lanes = basis_refs[0].shape[-1] // tile[1]
    weight = [
        [jnp.tile(inverse[j][k] / scale, (1, lanes)) if j <= k else None for k in range(size)]
        for j in range(size)
    ]

    def plane(i, carry):
        parts = [basis_refs[j][i] for j in range(size)]
        for k in range(size):
            acc = parts[0] * weight[0][k]
            for j in range(1, k + 1):
                acc = acc + parts[j] * weight[j][k]
            ortho_ref[k, i] = acc
        return carry

    lax.fori_loop(0, basis_refs[0].shape[0], plane, 0)


def finish(stats, basis, cells):
    size = len(basis)
    vmem = pl.BlockSpec(memory_space=pltpu.VMEM)
    ortho, upper, scale = pl.pallas_call(
        lambda *refs: finish_kernel(float(cells), size, *refs),
        out_shape=(
            jax.ShapeDtypeStruct((size,) + basis[0].shape, jnp.float32),
            jax.ShapeDtypeStruct((size, size), jnp.float32),
            jax.ShapeDtypeStruct((1, 1), jnp.float32),
        ),
        in_specs=[pl.BlockSpec(memory_space=pltpu.SMEM)] + [vmem] * size,
        out_specs=(vmem, vmem, vmem),
    )(stats, *basis)
    return ortho, upper, scale.reshape(())


def local(start_field, right_side, accumulation, trans_x, trans_y, trans_z):
    size_x, size_y, size_z = start_field.shape
    cells = size_x * size_y * size_z * lax.axis_size("gx") * lax.axis_size("gy")

    messages = lax.optimization_barrier((
        jnp.concatenate([start_field[:1], trans_x[:1]], axis=0),
        jnp.concatenate([start_field[-1:], trans_x[-1:]], axis=0),
        jnp.concatenate([start_field[:, :1], trans_y[:, :1]], axis=1),
        jnp.concatenate([start_field[:, -1:], trans_y[:, -1:]], axis=1),
    ))
    lo_both_x, hi_both_x, lo_both_y, hi_both_y = exchange(*messages)
    lo_x, hi_x, plane_x = lo_both_x[:1], hi_both_x[:1], hi_both_x[1:]
    lo_y, hi_y, plane_y = lo_both_y[:, :1], hi_both_y[:, :1], hi_both_y[:, 1:]

    zero_plane = jnp.zeros_like(trans_z[..., :1])
    tx_lo = trans_x
    tx_hi = jnp.concatenate([trans_x[1:], plane_x], axis=0)
    ty_lo = trans_y
    ty_hi = jnp.concatenate([trans_y[:, 1:], plane_y], axis=1)
    tz_lo = trans_z
    tz_hi = jnp.concatenate([trans_z[..., 1:], zero_plane], axis=-1)
    coef = (tx_lo, tx_hi, ty_lo, ty_hi, tz_lo, tz_hi)
    diagonal = accumulation + tx_lo + tx_hi + ty_lo + ty_hi + tz_lo + tz_hi

    total = neighbour_sum(start_field, (lo_x, hi_x, lo_y, hi_y), coef)
    residual0 = right_side - (diagonal * start_field - total)

    vector = residual0
    basis = [vector]
    for step in range(STEPS):
        total = neighbour_sum(vector, field_halo(vector), coef)
        vector = 2.0 * total / diagonal
        basis.append(vector)
    stats = gram(basis)
    stats = all_sum(stats)
    ortho, upper, scale = finish(stats, basis, cells)
    return (ortho, upper, scale)


def solution(mesh):
    in_specs = (
        P("gx", "gy", None),
        P("gx", "gy", None),
        P("gx", "gy", None),
        P("gx", "gy", None),
        P("gx", "gy", None),
        P("gx", "gy", None),
    )
    out_specs = (P(None, "gx", "gy", None), P(), P())
    return jax.shard_map(local, mesh=mesh, in_specs=in_specs, out_specs=out_specs, check_vma=False)
```

```python
import jax
import jax.numpy as jnp
from jax import lax
from jax.sharding import PartitionSpec as P
from jax.experimental import pallas as pl
from jax.experimental.pallas import tpu as pltpu

STEPS = 4


EPS = 1e-06


def shift_pairs(axis, by):
    peers = lax.axis_size(axis)
    return [(i, i + by) for i in range(peers) if 0 <= i + by < peers]


def swap_pairs(axis, parity):
    peers = lax.axis_size(axis)
    pairs = []
    for i in range(parity, peers - 1, 2):
        pairs += [(i, i + 1), (i + 1, i)]
    return pairs


def axis_exchange(to_low, to_high, axis):
    odd = lax.axis_index(axis) % 2 == 1
    even_swap = lax.ppermute(jnp.where(odd, to_low, to_high), axis, swap_pairs(axis, 0))
    odd_swap = lax.ppermute(jnp.where(odd, to_high, to_low), axis, swap_pairs(axis, 1))
    from_low = jnp.where(odd, even_swap, odd_swap)
    from_high = jnp.where(odd, odd_swap, even_swap)
    return from_low, from_high


def exchange(to_low_x, to_high_x, to_low_y, to_high_y):
    from_low_x, from_high_x = axis_exchange(to_low_x, to_high_x, "gx")
    from_low_y, from_high_y = axis_exchange(to_low_y, to_high_y, "gy")
    return from_low_x, from_high_x, from_low_y, from_high_y


def neighbour_sum(u, halo, coef):
    lo_x, hi_x, lo_y, hi_y = halo
    tx_lo, tx_hi, ty_lo, ty_hi, tz_lo, tz_hi = coef
    zero_plane = jnp.zeros_like(u[..., :1])
    u_xm = jnp.concatenate([lo_x, u[:-1]], axis=0)
    u_xp = jnp.concatenate([u[1:], hi_x], axis=0)
    u_ym = jnp.concatenate([lo_y, u[:, :-1]], axis=1)
    u_yp = jnp.concatenate([u[:, 1:], hi_y], axis=1)
    u_zm = jnp.concatenate([zero_plane, u[..., :-1]], axis=-1)
    u_zp = jnp.concatenate([u[..., 1:], zero_plane], axis=-1)
    total = tx_lo * u_xm + tx_hi * u_xp
    total = total + ty_lo * u_ym + ty_hi * u_yp
    total = total + tz_lo * u_zm + tz_hi * u_zp
    return total


def field_halo(u):
    return exchange(u[:1], u[-1:], u[:, :1], u[:, -1:])


def all_sum(x):
    for axis in ("gy", "gx"):
        n = lax.axis_size(axis)
        if n & (n - 1):
            x = lax.psum(x, axis)
            continue
        step = 1
        while step < n:
            x = x + lax.ppermute(x, axis, [(i, i ^ step) for i in range(n)])
            step *= 2
    return x


def gram_kernel(size, *refs):
    basis_refs, out_ref = refs[:size], refs[size]
    tile = out_ref.shape
    pairs = [(a, b) for a in range(size) for b in range(a, size)]
    planes, rows, lanes = basis_refs[0].shape
    chunks = lanes // tile[1]

    def plane(i, accs):
        accs = list(accs)
        for c in range(chunks):
            parts = [r[i, :, c * tile[1] : (c + 1) * tile[1]] for r in basis_refs]
            for n, (a, b) in enumerate(pairs):
                accs[n] = accs[n] + parts[a] * parts[b]
        return tuple(accs)

    zero = jnp.zeros((rows, tile[1]), jnp.float32)
    accs = lax.fori_loop(0, planes, plane, tuple(zero for _ in pairs))
    row_ids = lax.broadcasted_iota(jnp.int32, tile, 0)
    lane_ids = lax.broadcasted_iota(jnp.int32, tile, 1)
    packed = jnp.zeros(tile, jnp.float32)
    for n, (a, b) in enumerate(pairs):
        total = jnp.sum(accs[n])
        hit = (lane_ids == 1 + a * size + b) | (lane_ids == 1 + b * size + a)
        if a == 0 and b == 0:
            hit = hit | (lane_ids == 0)
        packed = jnp.where((row_ids == 0) & hit, total, packed)
    out_ref[...] = packed


def gram(basis):
    size = len(basis)
    vmem = pl.BlockSpec(memory_space=pltpu.VMEM)
    return pl.pallas_call(
        lambda *refs: gram_kernel(size, *refs),
        out_shape=jax.ShapeDtypeStruct((8, 128), jnp.float32),
        in_specs=[vmem] * size,
        out_specs=vmem,
    )(*basis)


def finish_kernel(cells, size, stats_ref, *refs):
    sources, (ortho_ref, upper_ref, scale_ref, held_basis, arrived) = refs[:size], refs[size:]
    copies = [pltpu.make_async_copy(sources[j], held_basis.at[j], arrived.at[j]) for j in range(size)]
    for copy in copies:
        copy.start()
    tile = (8, 128)

    def held(i):
        return jnp.full(tile, stats_ref[0, i], jnp.float32)

    scale = jnp.sqrt(held(0) / cells + EPS)
    square = scale * scale
    gram = [[held(1 + a * size + b) / cells / square for b in range(size)] for a in range(size)]
    upper = [[None] * size for _ in range(size)]
    for row in range(size):
        value = gram[row][row]
        for prev in range(row):
            value = value - upper[prev][row] * upper[prev][row]
        pivot = jnp.sqrt(value)
        upper[row][row] = pivot
        for col in range(row + 1, size):
            value = gram[row][col]
            for prev in range(row):
                value = value - upper[prev][row] * upper[prev][col]
            upper[row][col] = value / pivot
    inverse = [[None] * size for _ in range(size)]
    for col in range(size):
        for row in reversed(range(col + 1)):
            value = jnp.full(tile, 1.0 if row == col else 0.0, jnp.float32)
            for inner in range(row + 1, col + 1):
                value = value - upper[row][inner] * inverse[inner][col]
            inverse[row][col] = value / upper[row][row]
    rows = lax.broadcasted_iota(jnp.int32, tile, 0)
    cols = lax.broadcasted_iota(jnp.int32, tile, 1)
    packed = jnp.zeros(tile, jnp.float32)
    for row in range(size):
        for col in range(row, size):
            packed = jnp.where((rows == row) & (cols == col), upper[row][col], packed)
    upper_ref[...] = packed[: upper_ref.shape[0], : upper_ref.shape[1]]
    scale_ref[...] = scale[:1, :1]
    lanes = held_basis.shape[-1] // tile[1]
    weight = [
        [jnp.tile(inverse[j][k] / scale, (1, lanes)) if j <= k else None for k in range(size)]
        for j in range(size)
    ]

    for copy in copies:
        copy.wait()

    def plane(i, carry):
        parts = [held_basis[j, i] for j in range(size)]
        for k in range(size):
            acc = parts[0] * weight[0][k]
            for j in range(1, k + 1):
                acc = acc + parts[j] * weight[j][k]
            ortho_ref[k, i] = acc
        return carry

    lax.fori_loop(0, held_basis.shape[1], plane, 0)


def finish(stats, basis, cells):
    size = len(basis)
    vmem = pl.BlockSpec(memory_space=pltpu.VMEM)
    ortho, upper, scale = pl.pallas_call(
        lambda *refs: finish_kernel(float(cells), size, *refs),
        out_shape=(
            jax.ShapeDtypeStruct((size,) + basis[0].shape, jnp.float32),
            jax.ShapeDtypeStruct((size, size), jnp.float32),
            jax.ShapeDtypeStruct((1, 1), jnp.float32),
        ),
        in_specs=[pl.BlockSpec(memory_space=pltpu.SMEM)] + [pl.BlockSpec(memory_space=pl.ANY)] * size,
        out_specs=(vmem, vmem, vmem),
        scratch_shapes=[pltpu.VMEM((size,) + basis[0].shape, jnp.float32), pltpu.SemaphoreType.DMA((size,))],
    )(stats, *basis)
    return ortho, upper, scale.reshape(())


def local(start_field, right_side, accumulation, trans_x, trans_y, trans_z):
    size_x, size_y, size_z = start_field.shape
    cells = size_x * size_y * size_z * lax.axis_size("gx") * lax.axis_size("gy")

    lo_both_x, hi_both_x, lo_both_y, hi_both_y = exchange(
        jnp.concatenate([start_field[:1], trans_x[:1]], axis=0),
        jnp.concatenate([start_field[-1:], trans_x[-1:]], axis=0),
        jnp.concatenate([start_field[:, :1], trans_y[:, :1]], axis=1),
        jnp.concatenate([start_field[:, -1:], trans_y[:, -1:]], axis=1),
    )
    lo_x, hi_x, plane_x = lo_both_x[:1], hi_both_x[:1], hi_both_x[1:]
    lo_y, hi_y, plane_y = lo_both_y[:, :1], hi_both_y[:, :1], hi_both_y[:, 1:]

    zero_plane = jnp.zeros_like(trans_z[..., :1])
    tx_lo = trans_x
    tx_hi = jnp.concatenate([trans_x[1:], plane_x], axis=0)
    ty_lo = trans_y
    ty_hi = jnp.concatenate([trans_y[:, 1:], plane_y], axis=1)
    tz_lo = trans_z
    tz_hi = jnp.concatenate([trans_z[..., 1:], zero_plane], axis=-1)
    coef = (tx_lo, tx_hi, ty_lo, ty_hi, tz_lo, tz_hi)
    diagonal = accumulation + tx_lo + tx_hi + ty_lo + ty_hi + tz_lo + tz_hi

    total = neighbour_sum(start_field, (lo_x, hi_x, lo_y, hi_y), coef)
    residual0 = right_side - (diagonal * start_field - total)

    vector = residual0
    basis = [vector]
    for step in range(STEPS):
        total = neighbour_sum(vector, field_halo(vector), coef)
        vector = 2.0 * total / diagonal
        basis.append(vector)
    stats = gram(basis)
    stats = all_sum(stats)
    ortho, upper, scale = finish(stats, basis, cells)
    return (ortho, upper, scale)


def solution(mesh):
    in_specs = (
        P("gx", "gy", None),
        P("gx", "gy", None),
        P("gx", "gy", None),
        P("gx", "gy", None),
        P("gx", "gy", None),
        P("gx", "gy", None),
    )
    out_specs = (P(None, "gx", "gy", None), P(), P())
    return jax.shard_map(local, mesh=mesh, in_specs=in_specs, out_specs=out_specs, check_vma=False)
```

```python
import jax
import jax.numpy as jnp
from jax import lax
from jax.sharding import PartitionSpec as P
from jax.experimental import pallas as pl
from jax.experimental.pallas import tpu as pltpu

STEPS = 4


EPS = 1e-06


def shift_pairs(axis, by):
    peers = lax.axis_size(axis)
    return [(i, i + by) for i in range(peers) if 0 <= i + by < peers]


def swap_pairs(axis, parity):
    peers = lax.axis_size(axis)
    pairs = []
    for i in range(parity, peers - 1, 2):
        pairs += [(i, i + 1), (i + 1, i)]
    return pairs


def axis_exchange(to_low, to_high, axis):
    odd = lax.axis_index(axis) % 2 == 1
    even_swap = lax.ppermute(jnp.where(odd, to_low, to_high), axis, swap_pairs(axis, 0))
    odd_swap = lax.ppermute(jnp.where(odd, to_high, to_low), axis, swap_pairs(axis, 1))
    from_low = jnp.where(odd, even_swap, odd_swap)
    from_high = jnp.where(odd, odd_swap, even_swap)
    return from_low, from_high


def exchange(to_low_x, to_high_x, to_low_y, to_high_y):
    from_low_x, from_high_x = axis_exchange(to_low_x, to_high_x, "gx")
    from_low_y, from_high_y = axis_exchange(to_low_y, to_high_y, "gy")
    return from_low_x, from_high_x, from_low_y, from_high_y


def neighbour_sum(u, halo, coef):
    lo_x, hi_x, lo_y, hi_y = halo
    tx_lo, tx_hi, ty_lo, ty_hi, tz_lo, tz_hi = coef
    zero_plane = jnp.zeros_like(u[..., :1])
    u_xm = jnp.concatenate([lo_x, u[:-1]], axis=0)
    u_xp = jnp.concatenate([u[1:], hi_x], axis=0)
    u_ym = jnp.concatenate([lo_y, u[:, :-1]], axis=1)
    u_yp = jnp.concatenate([u[:, 1:], hi_y], axis=1)
    u_zm = jnp.concatenate([zero_plane, u[..., :-1]], axis=-1)
    u_zp = jnp.concatenate([u[..., 1:], zero_plane], axis=-1)
    total = tx_lo * u_xm + tx_hi * u_xp
    total = total + ty_lo * u_ym + ty_hi * u_yp
    total = total + tz_lo * u_zm + tz_hi * u_zp
    return total


def field_halo(u):
    lo_x, hi_x, lo_y, hi_y = exchange(u[:1], u[-1:], u[:, 0], u[:, -1])
    return lo_x, hi_x, lo_y[:, None], hi_y[:, None]


def all_sum(x):
    for axis in ("gy", "gx"):
        n = lax.axis_size(axis)
        if n & (n - 1):
            x = lax.psum(x, axis)
            continue
        step = 1
        while step < n:
            x = x + lax.ppermute(x, axis, [(i, i ^ step) for i in range(n)])
            step *= 2
    return x


def gram_kernel(size, *refs):
    basis_refs, out_ref = refs[:size], refs[size]
    tile = out_ref.shape
    pairs = [(a, b) for a in range(size) for b in range(a, size)]
    planes, rows, lanes = basis_refs[0].shape
    chunks = lanes // tile[1]

    def plane(i, accs):
        accs = list(accs)
        for c in range(chunks):
            parts = [r[i, :, c * tile[1] : (c + 1) * tile[1]] for r in basis_refs]
            for n, (a, b) in enumerate(pairs):
                accs[n] = accs[n] + parts[a] * parts[b]
        return tuple(accs)

    zero = jnp.zeros((rows, tile[1]), jnp.float32)
    accs = lax.fori_loop(0, planes, plane, tuple(zero for _ in pairs))
    row_ids = lax.broadcasted_iota(jnp.int32, tile, 0)
    lane_ids = lax.broadcasted_iota(jnp.int32, tile, 1)
    packed = jnp.zeros(tile, jnp.float32)
    for n, (a, b) in enumerate(pairs):
        total = jnp.sum(accs[n])
        hit = (lane_ids == 1 + a * size + b) | (lane_ids == 1 + b * size + a)
        if a == 0 and b == 0:
            hit = hit | (lane_ids == 0)
        packed = jnp.where((row_ids == 0) & hit, total, packed)
    out_ref[...] = packed


def gram(basis):
    size = len(basis)
    vmem = pl.BlockSpec(memory_space=pltpu.VMEM)
    return pl.pallas_call(
        lambda *refs: gram_kernel(size, *refs),
        out_shape=jax.ShapeDtypeStruct((8, 128), jnp.float32),
        in_specs=[vmem] * size,
        out_specs=vmem,
    )(*basis)


def finish_kernel(cells, size, stats_ref, *refs):
    basis_refs, (ortho_ref, upper_ref, scale_ref) = refs[:size], refs[size:]
    tile = (8, 128)

    def held(i):
        return jnp.full(tile, stats_ref[0, i], jnp.float32)

    scale = jnp.sqrt(held(0) / cells + EPS)
    square = scale * scale
    gram = [[held(1 + a * size + b) / cells / square for b in range(size)] for a in range(size)]
    upper = [[None] * size for _ in range(size)]
    for row in range(size):
        value = gram[row][row]
        for prev in range(row):
            value = value - upper[prev][row] * upper[prev][row]
        pivot = jnp.sqrt(value)
        upper[row][row] = pivot
        for col in range(row + 1, size):
            value = gram[row][col]
            for prev in range(row):
                value = value - upper[prev][row] * upper[prev][col]
            upper[row][col] = value / pivot
    inverse = [[None] * size for _ in range(size)]
    for col in range(size):
        for row in reversed(range(col + 1)):
            value = jnp.full(tile, 1.0 if row == col else 0.0, jnp.float32)
            for inner in range(row + 1, col + 1):
                value = value - upper[row][inner] * inverse[inner][col]
            inverse[row][col] = value / upper[row][row]
    rows = lax.broadcasted_iota(jnp.int32, tile, 0)
    cols = lax.broadcasted_iota(jnp.int32, tile, 1)
    packed = jnp.zeros(tile, jnp.float32)
    for row in range(size):
        for col in range(row, size):
            packed = jnp.where((rows == row) & (cols == col), upper[row][col], packed)
    upper_ref[...] = packed[: upper_ref.shape[0], : upper_ref.shape[1]]
    scale_ref[...] = scale[:1, :1]
    lanes = basis_refs[0].shape[-1] // tile[1]
    weight = [
        [jnp.tile(inverse[j][k] / scale, (1, lanes)) if j <= k else None for k in range(size)]
        for j in range(size)
    ]

    def plane(i, carry):
        parts = [basis_refs[j][i] for j in range(size)]
        for k in range(size):
            acc = parts[0] * weight[0][k]
            for j in range(1, k + 1):
                acc = acc + parts[j] * weight[j][k]
            ortho_ref[k, i] = acc
        return carry

    lax.fori_loop(0, basis_refs[0].shape[0], plane, 0)


def finish(stats, basis, cells):
    size = len(basis)
    vmem = pl.BlockSpec(memory_space=pltpu.VMEM)
    ortho, upper, scale = pl.pallas_call(
        lambda *refs: finish_kernel(float(cells), size, *refs),
        out_shape=(
            jax.ShapeDtypeStruct((size,) + basis[0].shape, jnp.float32),
            jax.ShapeDtypeStruct((size, size), jnp.float32),
            jax.ShapeDtypeStruct((1, 1), jnp.float32),
        ),
        in_specs=[pl.BlockSpec(memory_space=pltpu.SMEM)] + [vmem] * size,
        out_specs=(vmem, vmem, vmem),
    )(stats, *basis)
    return ortho, upper, scale.reshape(())


def local(start_field, right_side, accumulation, trans_x, trans_y, trans_z):
    size_x, size_y, size_z = start_field.shape
    cells = size_x * size_y * size_z * lax.axis_size("gx") * lax.axis_size("gy")

    lo_both_x, hi_both_x, lo_both_y, hi_both_y = exchange(
        jnp.concatenate([start_field[:1], trans_x[:1]], axis=0),
        jnp.concatenate([start_field[-1:], trans_x[-1:]], axis=0),
        jnp.concatenate([start_field[:, 0], trans_y[:, 0]], axis=0),
        jnp.concatenate([start_field[:, -1], trans_y[:, -1]], axis=0),
    )
    size_x = start_field.shape[0]
    lo_x, hi_x, plane_x = lo_both_x[:1], hi_both_x[:1], hi_both_x[1:]
    lo_y, hi_y, plane_y = (a[:, None] for a in (lo_both_y[:size_x], hi_both_y[:size_x], hi_both_y[size_x:]))

    zero_plane = jnp.zeros_like(trans_z[..., :1])
    tx_lo = trans_x
    tx_hi = jnp.concatenate([trans_x[1:], plane_x], axis=0)
    ty_lo = trans_y
    ty_hi = jnp.concatenate([trans_y[:, 1:], plane_y], axis=1)
    tz_lo = trans_z
    tz_hi = jnp.concatenate([trans_z[..., 1:], zero_plane], axis=-1)
    coef = (tx_lo, tx_hi, ty_lo, ty_hi, tz_lo, tz_hi)
    diagonal = accumulation + tx_lo + tx_hi + ty_lo + ty_hi + tz_lo + tz_hi

    total = neighbour_sum(start_field, (lo_x, hi_x, lo_y, hi_y), coef)
    residual0 = right_side - (diagonal * start_field - total)

    vector = residual0
    basis = [vector]
    for step in range(STEPS):
        total = neighbour_sum(vector, field_halo(vector), coef)
        vector = 2.0 * total / diagonal
        basis.append(vector)
    stats = gram(basis)
    stats = all_sum(stats)
    ortho, upper, scale = finish(stats, basis, cells)
    return (ortho, upper, scale)


def solution(mesh):
    in_specs = (
        P("gx", "gy", None),
        P("gx", "gy", None),
        P("gx", "gy", None),
        P("gx", "gy", None),
        P("gx", "gy", None),
        P("gx", "gy", None),
    )
    out_specs = (P(None, "gx", "gy", None), P(), P())
    return jax.shard_map(local, mesh=mesh, in_specs=in_specs, out_specs=out_specs, check_vma=False)
```

```python
import jax
import jax.numpy as jnp
from jax import lax
from jax.sharding import PartitionSpec as P
from jax.experimental import pallas as pl
from jax.experimental.pallas import tpu as pltpu

STEPS = 4


EPS = 1e-06


def shift_pairs(axis, by):
    peers = lax.axis_size(axis)
    return [(i, i + by) for i in range(peers) if 0 <= i + by < peers]


def swap_pairs(axis, parity):
    peers = lax.axis_size(axis)
    pairs = []
    for i in range(parity, peers - 1, 2):
        pairs += [(i, i + 1), (i + 1, i)]
    return pairs


def axis_exchange(to_low, to_high, axis):
    odd = lax.axis_index(axis) % 2 == 1
    even_swap = lax.ppermute(jnp.where(odd, to_low, to_high), axis, swap_pairs(axis, 0))
    odd_swap = lax.ppermute(jnp.where(odd, to_high, to_low), axis, swap_pairs(axis, 1))
    from_low = jnp.where(odd, even_swap, odd_swap)
    from_high = jnp.where(odd, odd_swap, even_swap)
    return from_low, from_high


def exchange(to_low_x, to_high_x, to_low_y, to_high_y):
    from_low_x, from_high_x = axis_exchange(to_low_x, to_high_x, "gx")
    from_low_y, from_high_y = axis_exchange(to_low_y, to_high_y, "gy")
    return from_low_x, from_high_x, from_low_y, from_high_y


def neighbour_sum(u, halo, coef):
    lo_x, hi_x, lo_y, hi_y = halo
    tx_lo, tx_hi, ty_lo, ty_hi, tz_lo, tz_hi = coef
    zero_plane = jnp.zeros_like(u[..., :1])
    u_xm = jnp.concatenate([lo_x, u[:-1]], axis=0)
    u_xp = jnp.concatenate([u[1:], hi_x], axis=0)
    u_ym = jnp.concatenate([lo_y, u[:, :-1]], axis=1)
    u_yp = jnp.concatenate([u[:, 1:], hi_y], axis=1)
    u_zm = jnp.concatenate([zero_plane, u[..., :-1]], axis=-1)
    u_zp = jnp.concatenate([u[..., 1:], zero_plane], axis=-1)
    total = tx_lo * u_xm + tx_hi * u_xp
    total = total + ty_lo * u_ym + ty_hi * u_yp
    total = total + tz_lo * u_zm + tz_hi * u_zp
    return total


def field_halo(u):
    return exchange(u[:1], u[-1:], u[:, :1], u[:, -1:])


def all_sum(x):
    for axis in ("gy", "gx"):
        n = lax.axis_size(axis)
        if n & (n - 1):
            x = lax.psum(x, axis)
            continue
        step = 1
        while step < n:
            x = x + lax.ppermute(x, axis, [(i, i ^ step) for i in range(n)])
            step *= 2
    return x


def gram_kernel(size, *refs):
    basis_refs, out_ref = refs[:size], refs[size]
    tile = out_ref.shape
    pairs = [(a, b) for a in range(size) for b in range(a, size)]
    planes, rows, lanes = basis_refs[0].shape
    chunks = lanes // tile[1]

    def plane(i, accs):
        accs = list(accs)
        for c in range(chunks):
            parts = [r[i, :, c * tile[1] : (c + 1) * tile[1]] for r in basis_refs]
            for n, (a, b) in enumerate(pairs):
                accs[n] = accs[n] + parts[a] * parts[b]
        return tuple(accs)

    zero = jnp.zeros((rows, tile[1]), jnp.float32)
    accs = lax.fori_loop(0, planes, plane, tuple(zero for _ in pairs))
    row_ids = lax.broadcasted_iota(jnp.int32, tile, 0)
    lane_ids = lax.broadcasted_iota(jnp.int32, tile, 1)
    packed = jnp.zeros(tile, jnp.float32)
    for n, (a, b) in enumerate(pairs):
        total = jnp.sum(accs[n])
        hit = (lane_ids == 1 + a * size + b) | (lane_ids == 1 + b * size + a)
        if a == 0 and b == 0:
            hit = hit | (lane_ids == 0)
        packed = jnp.where((row_ids == 0) & hit, total, packed)
    out_ref[...] = packed


def gram(basis):
    size = len(basis)
    vmem = pl.BlockSpec(memory_space=pltpu.VMEM)
    return pl.pallas_call(
        lambda *refs: gram_kernel(size, *refs),
        out_shape=jax.ShapeDtypeStruct((8, 128), jnp.float32),
        in_specs=[vmem] * size,
        out_specs=vmem,
    )(*basis)


def finish_kernel(cells, size, stats_ref, *refs):
    basis_refs, (ortho_ref, upper_ref, scale_ref) = refs[:size], refs[size:]
    tile = (8, 128)

    def held(i):
        return jnp.full(tile, stats_ref[0, i], jnp.float32)

    per_cell = 1.0 / cells
    scale = jnp.sqrt(held(0) * per_cell + EPS)
    unscale = 1.0 / scale
    weight_g = per_cell * (unscale * unscale)
    gram = [[held(1 + a * size + b) * weight_g for b in range(size)] for a in range(size)]
    upper = [[None] * size for _ in range(size)]
    recip = [None] * size
    for row in range(size):
        value = gram[row][row]
        for prev in range(row):
            value = value - upper[prev][row] * upper[prev][row]
        pivot = jnp.sqrt(value)
        upper[row][row] = pivot
        recip[row] = 1.0 / pivot
        for col in range(row + 1, size):
            value = gram[row][col]
            for prev in range(row):
                value = value - upper[prev][row] * upper[prev][col]
            upper[row][col] = value * recip[row]
    inverse = [[None] * size for _ in range(size)]
    for col in range(size):
        for row in reversed(range(col + 1)):
            if row == col:
                inverse[row][col] = recip[row]
                continue
            value = jnp.zeros(tile, jnp.float32)
            for inner in range(row + 1, col + 1):
                value = value - upper[row][inner] * inverse[inner][col]
            inverse[row][col] = value * recip[row]
    rows = lax.broadcasted_iota(jnp.int32, tile, 0)
    cols = lax.broadcasted_iota(jnp.int32, tile, 1)
    packed = jnp.zeros(tile, jnp.float32)
    for row in range(size):
        for col in range(row, size):
            packed = jnp.where((rows == row) & (cols == col), upper[row][col], packed)
    upper_ref[...] = packed[: upper_ref.shape[0], : upper_ref.shape[1]]
    scale_ref[...] = scale[:1, :1]
    lanes = basis_refs[0].shape[-1] // tile[1]
    weight = [
        [jnp.tile(inverse[j][k] * unscale, (1, lanes)) if j <= k else None for k in range(size)]
        for j in range(size)
    ]

    def plane(i, carry):
        parts = [basis_refs[j][i] for j in range(size)]
        for k in range(size):
            acc = parts[0] * weight[0][k]
            for j in range(1, k + 1):
                acc = acc + parts[j] * weight[j][k]
            ortho_ref[k, i] = acc
        return carry

    lax.fori_loop(0, basis_refs[0].shape[0], plane, 0)


def finish(stats, basis, cells):
    size = len(basis)
    vmem = pl.BlockSpec(memory_space=pltpu.VMEM)
    ortho, upper, scale = pl.pallas_call(
        lambda *refs: finish_kernel(float(cells), size, *refs),
        out_shape=(
            jax.ShapeDtypeStruct((size,) + basis[0].shape, jnp.float32),
            jax.ShapeDtypeStruct((size, size), jnp.float32),
            jax.ShapeDtypeStruct((1, 1), jnp.float32),
        ),
        in_specs=[pl.BlockSpec(memory_space=pltpu.SMEM)] + [vmem] * size,
        out_specs=(vmem, vmem, vmem),
    )(stats, *basis)
    return ortho, upper, scale.reshape(())


def local(start_field, right_side, accumulation, trans_x, trans_y, trans_z):
    size_x, size_y, size_z = start_field.shape
    cells = size_x * size_y * size_z * lax.axis_size("gx") * lax.axis_size("gy")

    lo_both_x, hi_both_x, lo_both_y, hi_both_y = exchange(
        jnp.concatenate([start_field[:1], trans_x[:1]], axis=0),
        jnp.concatenate([start_field[-1:], trans_x[-1:]], axis=0),
        jnp.concatenate([start_field[:, :1], trans_y[:, :1]], axis=1),
        jnp.concatenate([start_field[:, -1:], trans_y[:, -1:]], axis=1),
    )
    lo_x, hi_x, plane_x = lo_both_x[:1], hi_both_x[:1], hi_both_x[1:]
    lo_y, hi_y, plane_y = lo_both_y[:, :1], hi_both_y[:, :1], hi_both_y[:, 1:]

    zero_plane = jnp.zeros_like(trans_z[..., :1])
    tx_lo = trans_x
    tx_hi = jnp.concatenate([trans_x[1:], plane_x], axis=0)
    ty_lo = trans_y
    ty_hi = jnp.concatenate([trans_y[:, 1:], plane_y], axis=1)
    tz_lo = trans_z
    tz_hi = jnp.concatenate([trans_z[..., 1:], zero_plane], axis=-1)
    coef = (tx_lo, tx_hi, ty_lo, ty_hi, tz_lo, tz_hi)
    diagonal = accumulation + tx_lo + tx_hi + ty_lo + ty_hi + tz_lo + tz_hi

    total = neighbour_sum(start_field, (lo_x, hi_x, lo_y, hi_y), coef)
    residual0 = right_side - (diagonal * start_field - total)

    vector = residual0
    basis = [vector]
    for step in range(STEPS):
        total = neighbour_sum(vector, field_halo(vector), coef)
        vector = 2.0 * total / diagonal
        basis.append(vector)
    stats = gram(basis)
    stats = all_sum(stats)
    ortho, upper, scale = finish(stats, basis, cells)
    return (ortho, upper, scale)


def solution(mesh):
    in_specs = (
        P("gx", "gy", None),
        P("gx", "gy", None),
        P("gx", "gy", None),
        P("gx", "gy", None),
        P("gx", "gy", None),
        P("gx", "gy", None),
    )
    out_specs = (P(None, "gx", "gy", None), P(), P())
    return jax.shard_map(local, mesh=mesh, in_specs=in_specs, out_specs=out_specs, check_vma=False)
```

```python
import jax
import jax.numpy as jnp
from jax import lax
from jax.sharding import PartitionSpec as P
from jax.experimental import pallas as pl
from jax.experimental.pallas import tpu as pltpu

STEPS = 4


EPS = 1e-06


def shift_pairs(axis, by):
    peers = lax.axis_size(axis)
    return [(i, i + by) for i in range(peers) if 0 <= i + by < peers]


def swap_pairs(axis, parity):
    peers = lax.axis_size(axis)
    pairs = []
    for i in range(parity, peers - 1, 2):
        pairs += [(i, i + 1), (i + 1, i)]
    return pairs


def axis_exchange(to_low, to_high, axis):
    odd = lax.axis_index(axis) % 2 == 1
    even_swap = lax.ppermute(jnp.where(odd, to_low, to_high), axis, swap_pairs(axis, 0))
    odd_swap = lax.ppermute(jnp.where(odd, to_high, to_low), axis, swap_pairs(axis, 1))
    from_low = jnp.where(odd, even_swap, odd_swap)
    from_high = jnp.where(odd, odd_swap, even_swap)
    return from_low, from_high


def exchange(to_low_x, to_high_x, to_low_y, to_high_y):
    from_low_x, from_high_x = axis_exchange(to_low_x, to_high_x, "gx")
    from_low_y, from_high_y = axis_exchange(to_low_y, to_high_y, "gy")
    return from_low_x, from_high_x, from_low_y, from_high_y


def neighbour_sum(u, halo, coef):
    lo_x, hi_x, lo_y, hi_y = halo
    tx_lo, tx_hi, ty_lo, ty_hi, tz_lo, tz_hi = coef
    zero_plane = jnp.zeros_like(u[..., :1])
    u_xm = jnp.concatenate([lo_x, u[:-1]], axis=0)
    u_xp = jnp.concatenate([u[1:], hi_x], axis=0)
    u_ym = jnp.concatenate([lo_y, u[:, :-1]], axis=1)
    u_yp = jnp.concatenate([u[:, 1:], hi_y], axis=1)
    u_zm = jnp.concatenate([zero_plane, u[..., :-1]], axis=-1)
    u_zp = jnp.concatenate([u[..., 1:], zero_plane], axis=-1)
    total = tx_lo * u_xm + tx_hi * u_xp
    total = total + ty_lo * u_ym + ty_hi * u_yp
    total = total + tz_lo * u_zm + tz_hi * u_zp
    return total


def field_halo(u):
    return exchange(u[:1], u[-1:], u[:, :1], u[:, -1:])


def all_sum(x):
    for axis in ("gy", "gx"):
        n = lax.axis_size(axis)
        if n & (n - 1):
            x = lax.psum(x, axis)
            continue
        step = 1
        while step < n:
            x = x + lax.ppermute(x, axis, [(i, i ^ step) for i in range(n)])
            step *= 2
    return x


def gram_kernel(size, *refs):
    basis_refs, out_ref = refs[:size], refs[size]
    tile = out_ref.shape
    pairs = [(a, b) for a in range(size) for b in range(a, size)]
    planes, rows, lanes = basis_refs[0].shape
    chunks = lanes // tile[1]

    def plane(i, accs):
        accs = list(accs)
        for c in range(chunks):
            parts = [r[i, :, c * tile[1] : (c + 1) * tile[1]] for r in basis_refs]
            for n, (a, b) in enumerate(pairs):
                accs[n] = accs[n] + parts[a] * parts[b]
        return tuple(accs)

    zero = jnp.zeros((rows, tile[1]), jnp.float32)
    accs = lax.fori_loop(0, planes, plane, tuple(zero for _ in pairs))
    row_ids = lax.broadcasted_iota(jnp.int32, tile, 0)
    lane_ids = lax.broadcasted_iota(jnp.int32, tile, 1)
    packed = jnp.zeros(tile, jnp.float32)
    for n, (a, b) in enumerate(pairs):
        total = jnp.sum(accs[n])
        hit = (lane_ids == 1 + a * size + b) | (lane_ids == 1 + b * size + a)
        if a == 0 and b == 0:
            hit = hit | (lane_ids == 0)
        packed = jnp.where((row_ids == 0) & hit, total, packed)
    out_ref[...] = packed


def gram(basis):
    size = len(basis)
    vmem = pl.BlockSpec(memory_space=pltpu.VMEM)
    return pl.pallas_call(
        lambda *refs: gram_kernel(size, *refs),
        out_shape=jax.ShapeDtypeStruct((8, 128), jnp.float32),
        in_specs=[vmem] * size,
        out_specs=vmem,
    )(*basis)


def finish_kernel(cells, size, stats_ref, *refs):
    basis_refs, (ortho_ref, upper_ref, scale_ref) = refs[:size], refs[size:]
    tile = (8, 128)

    def held(i):
        return jnp.full(tile, stats_ref[0, i], jnp.float32)

    per_cell = 1.0 / cells
    scale = jnp.sqrt(held(0) * per_cell + EPS)
    unscale = 1.0 / scale
    weight_g = per_cell * (unscale * unscale)
    gram = [[held(1 + a * size + b) * weight_g for b in range(size)] for a in range(size)]
    upper = [[None] * size for _ in range(size)]
    recip = [None] * size
    for row in range(size):
        value = gram[row][row]
        for prev in range(row):
            value = value - upper[prev][row] * upper[prev][row]
        pivot = jnp.sqrt(value)
        upper[row][row] = pivot
        recip[row] = 1.0 / pivot
        for col in range(row + 1, size):
            value = gram[row][col]
            for prev in range(row):
                value = value - upper[prev][row] * upper[prev][col]
            upper[row][col] = value * recip[row]
    inverse = [[None] * size for _ in range(size)]
    for col in range(size):
        for row in reversed(range(col + 1)):
            if row == col:
                inverse[row][col] = recip[row]
                continue
            value = jnp.zeros(tile, jnp.float32)
            for inner in range(row + 1, col + 1):
                value = value - upper[row][inner] * inverse[inner][col]
            inverse[row][col] = value * recip[row]
    rows = lax.broadcasted_iota(jnp.int32, tile, 0)
    cols = lax.broadcasted_iota(jnp.int32, tile, 1)
    packed = jnp.zeros(tile, jnp.float32)
    for row in range(size):
        for col in range(row, size):
            packed = jnp.where((rows == row) & (cols == col), upper[row][col], packed)
    upper_ref[...] = packed[: upper_ref.shape[0], : upper_ref.shape[1]]
    scale_ref[...] = scale[:1, :1]
    lanes = basis_refs[0].shape[-1] // tile[1]
    weight = [
        [jnp.tile(inverse[j][k] * unscale, (1, lanes)) if j <= k else None for k in range(size)]
        for j in range(size)
    ]

    def plane(i, carry):
        parts = [basis_refs[j][i] for j in range(size)]
        for k in range(size):
            acc = parts[0] * weight[0][k]
            for j in range(1, k + 1):
                acc = acc + parts[j] * weight[j][k]
            ortho_ref[k, i] = acc
        return carry

    lax.fori_loop(0, basis_refs[0].shape[0], plane, 0)


def finish(stats, basis, cells):
    size = len(basis)
    planes, rows, lanes = basis[0].shape
    chunk = 4 if planes % 4 == 0 else planes
    part = pl.BlockSpec((chunk, rows, lanes), lambda i: (i, 0, 0))
    ortho, upper, scale = pl.pallas_call(
        lambda *refs: finish_kernel(float(cells), size, *refs),
        grid=(planes // chunk,),
        out_shape=(
            jax.ShapeDtypeStruct((size,) + basis[0].shape, jnp.float32),
            jax.ShapeDtypeStruct((size, size), jnp.float32),
            jax.ShapeDtypeStruct((1, 1), jnp.float32),
        ),
        in_specs=[pl.BlockSpec(memory_space=pltpu.SMEM)] + [part] * size,
        out_specs=(
            pl.BlockSpec((size, chunk, rows, lanes), lambda i: (0, i, 0, 0)),
            pl.BlockSpec((size, size), lambda i: (0, 0)),
            pl.BlockSpec((1, 1), lambda i: (0, 0)),
        ),
    )(stats, *basis)
    return ortho, upper, scale.reshape(())


def local(start_field, right_side, accumulation, trans_x, trans_y, trans_z):
    size_x, size_y, size_z = start_field.shape
    cells = size_x * size_y * size_z * lax.axis_size("gx") * lax.axis_size("gy")

    lo_both_x, hi_both_x, lo_both_y, hi_both_y = exchange(
        jnp.concatenate([start_field[:1], trans_x[:1]], axis=0),
        jnp.concatenate([start_field[-1:], trans_x[-1:]], axis=0),
        jnp.concatenate([start_field[:, :1], trans_y[:, :1]], axis=1),
        jnp.concatenate([start_field[:, -1:], trans_y[:, -1:]], axis=1),
    )
    lo_x, hi_x, plane_x = lo_both_x[:1], hi_both_x[:1], hi_both_x[1:]
    lo_y, hi_y, plane_y = lo_both_y[:, :1], hi_both_y[:, :1], hi_both_y[:, 1:]

    zero_plane = jnp.zeros_like(trans_z[..., :1])
    tx_lo = trans_x
    tx_hi = jnp.concatenate([trans_x[1:], plane_x], axis=0)
    ty_lo = trans_y
    ty_hi = jnp.concatenate([trans_y[:, 1:], plane_y], axis=1)
    tz_lo = trans_z
    tz_hi = jnp.concatenate([trans_z[..., 1:], zero_plane], axis=-1)
    coef = (tx_lo, tx_hi, ty_lo, ty_hi, tz_lo, tz_hi)
    diagonal = accumulation + tx_lo + tx_hi + ty_lo + ty_hi + tz_lo + tz_hi

    total = neighbour_sum(start_field, (lo_x, hi_x, lo_y, hi_y), coef)
    residual0 = right_side - (diagonal * start_field - total)

    vector = residual0
    basis = [vector]
    for step in range(STEPS):
        total = neighbour_sum(vector, field_halo(vector), coef)
        vector = 2.0 * total / diagonal
        basis.append(vector)
    stats = gram(basis)
    stats = all_sum(stats)
    ortho, upper, scale = finish(stats, basis, cells)
    return (ortho, upper, scale)


def solution(mesh):
    in_specs = (
        P("gx", "gy", None),
        P("gx", "gy", None),
        P("gx", "gy", None),
        P("gx", "gy", None),
        P("gx", "gy", None),
        P("gx", "gy", None),
    )
    out_specs = (P(None, "gx", "gy", None), P(), P())
    return jax.shard_map(local, mesh=mesh, in_specs=in_specs, out_specs=out_specs, check_vma=False)
```

```python
import jax
import jax.numpy as jnp
from jax import lax
from jax.sharding import PartitionSpec as P
from jax.experimental import pallas as pl
from jax.experimental.pallas import tpu as pltpu

STEPS = 4


EPS = 1e-06


def shift_pairs(axis, by):
    peers = lax.axis_size(axis)
    return [(i, i + by) for i in range(peers) if 0 <= i + by < peers]


def swap_pairs(axis, parity):
    peers = lax.axis_size(axis)
    pairs = []
    for i in range(parity, peers - 1, 2):
        pairs += [(i, i + 1), (i + 1, i)]
    return pairs


def axis_exchange(to_low, to_high, axis):
    odd = lax.axis_index(axis) % 2 == 1
    even_swap = lax.ppermute(jnp.where(odd, to_low, to_high), axis, swap_pairs(axis, 0))
    odd_swap = lax.ppermute(jnp.where(odd, to_high, to_low), axis, swap_pairs(axis, 1))
    from_low = jnp.where(odd, even_swap, odd_swap)
    from_high = jnp.where(odd, odd_swap, even_swap)
    return from_low, from_high


def exchange(to_low_x, to_high_x, to_low_y, to_high_y):
    from_low_x, from_high_x = axis_exchange(to_low_x, to_high_x, "gx")
    from_low_y, from_high_y = axis_exchange(to_low_y, to_high_y, "gy")
    return from_low_x, from_high_x, from_low_y, from_high_y


def neighbour_sum(u, halo, coef):
    lo_x, hi_x, lo_y, hi_y = halo
    tx_lo, tx_hi, ty_lo, ty_hi, tz_lo, tz_hi = coef
    zero_plane = jnp.zeros_like(u[..., :1])
    u_xm = jnp.concatenate([lo_x, u[:-1]], axis=0)
    u_xp = jnp.concatenate([u[1:], hi_x], axis=0)
    u_ym = jnp.concatenate([lo_y, u[:, :-1]], axis=1)
    u_yp = jnp.concatenate([u[:, 1:], hi_y], axis=1)
    u_zm = jnp.concatenate([zero_plane, u[..., :-1]], axis=-1)
    u_zp = jnp.concatenate([u[..., 1:], zero_plane], axis=-1)
    total = tx_lo * u_xm + tx_hi * u_xp
    total = total + ty_lo * u_ym + ty_hi * u_yp
    total = total + tz_lo * u_zm + tz_hi * u_zp
    return total


def field_halo(u):
    return exchange(u[:1], u[-1:], u[:, :1], u[:, -1:])


def all_sum(x):
    for axis in ("gy", "gx"):
        n = lax.axis_size(axis)
        if n & (n - 1):
            x = lax.psum(x, axis)
            continue
        step = 1
        while step < n:
            x = x + lax.ppermute(x, axis, [(i, i ^ step) for i in range(n)])
            step *= 2
    return x


def gram_kernel(size, *refs):
    basis_refs, out_ref = refs[:size], refs[size]
    tile = out_ref.shape
    pairs = [(a, b) for a in range(size) for b in range(a, size)]
    planes, rows, lanes = basis_refs[0].shape
    chunks = lanes // tile[1]

    def plane(i, accs):
        accs = list(accs)
        for c in range(chunks):
            parts = [r[i, :, c * tile[1] : (c + 1) * tile[1]] for r in basis_refs]
            for n, (a, b) in enumerate(pairs):
                accs[n] = accs[n] + parts[a] * parts[b]
        return tuple(accs)

    zero = jnp.zeros((rows, tile[1]), jnp.float32)
    accs = lax.fori_loop(0, planes, plane, tuple(zero for _ in pairs))
    row_ids = lax.broadcasted_iota(jnp.int32, tile, 0)
    lane_ids = lax.broadcasted_iota(jnp.int32, tile, 1)
    packed = jnp.zeros(tile, jnp.float32)
    for n, (a, b) in enumerate(pairs):
        total = jnp.sum(accs[n])
        hit = (lane_ids == 1 + a * size + b) | (lane_ids == 1 + b * size + a)
        if a == 0 and b == 0:
            hit = hit | (lane_ids == 0)
        packed = jnp.where((row_ids == 0) & hit, total, packed)
    out_ref[...] = packed


def gram(basis):
    size = len(basis)
    vmem = pl.BlockSpec(memory_space=pltpu.VMEM)
    return pl.pallas_call(
        lambda *refs: gram_kernel(size, *refs),
        out_shape=jax.ShapeDtypeStruct((1, 128), jnp.float32),
        in_specs=[vmem] * size,
        out_specs=vmem,
    )(*basis)


def finish_kernel(cells, size, stats_ref, *refs):
    basis_refs, (ortho_ref, upper_ref, scale_ref) = refs[:size], refs[size:]
    tile = (8, 128)

    def held(i):
        return jnp.full(tile, stats_ref[0, i], jnp.float32)

    per_cell = 1.0 / cells
    scale = jnp.sqrt(held(0) * per_cell + EPS)
    unscale = 1.0 / scale
    weight_g = per_cell * (unscale * unscale)
    gram = [[held(1 + a * size + b) * weight_g for b in range(size)] for a in range(size)]
    upper = [[None] * size for _ in range(size)]
    recip = [None] * size
    for row in range(size):
        value = gram[row][row]
        for prev in range(row):
            value = value - upper[prev][row] * upper[prev][row]
        pivot = jnp.sqrt(value)
        upper[row][row] = pivot
        recip[row] = 1.0 / pivot
        for col in range(row + 1, size):
            value = gram[row][col]
            for prev in range(row):
                value = value - upper[prev][row] * upper[prev][col]
            upper[row][col] = value * recip[row]
    inverse = [[None] * size for _ in range(size)]
    for col in range(size):
        for row in reversed(range(col + 1)):
            if row == col:
                inverse[row][col] = recip[row]
                continue
            value = jnp.zeros(tile, jnp.float32)
            for inner in range(row + 1, col + 1):
                value = value - upper[row][inner] * inverse[inner][col]
            inverse[row][col] = value * recip[row]
    rows = lax.broadcasted_iota(jnp.int32, tile, 0)
    cols = lax.broadcasted_iota(jnp.int32, tile, 1)
    packed = jnp.zeros(tile, jnp.float32)
    for row in range(size):
        for col in range(row, size):
            packed = jnp.where((rows == row) & (cols == col), upper[row][col], packed)
    upper_ref[...] = packed[: upper_ref.shape[0], : upper_ref.shape[1]]
    scale_ref[...] = scale[:1, :1]
    lanes = basis_refs[0].shape[-1] // tile[1]
    weight = [
        [jnp.tile(inverse[j][k] * unscale, (1, lanes)) if j <= k else None for k in range(size)]
        for j in range(size)
    ]

    def plane(i, carry):
        parts = [basis_refs[j][i] for j in range(size)]
        for k in range(size):
            acc = parts[0] * weight[0][k]
            for j in range(1, k + 1):
                acc = acc + parts[j] * weight[j][k]
            ortho_ref[k, i] = acc
        return carry

    lax.fori_loop(0, basis_refs[0].shape[0], plane, 0)


def finish(stats, basis, cells):
    size = len(basis)
    vmem = pl.BlockSpec(memory_space=pltpu.VMEM)
    ortho, upper, scale = pl.pallas_call(
        lambda *refs: finish_kernel(float(cells), size, *refs),
        out_shape=(
            jax.ShapeDtypeStruct((size,) + basis[0].shape, jnp.float32),
            jax.ShapeDtypeStruct((size, size), jnp.float32),
            jax.ShapeDtypeStruct((1, 1), jnp.float32),
        ),
        in_specs=[pl.BlockSpec(memory_space=pltpu.SMEM)] + [vmem] * size,
        out_specs=(vmem, vmem, vmem),
    )(stats, *basis)
    return ortho, upper, scale.reshape(())


def local(start_field, right_side, accumulation, trans_x, trans_y, trans_z):
    size_x, size_y, size_z = start_field.shape
    cells = size_x * size_y * size_z * lax.axis_size("gx") * lax.axis_size("gy")

    lo_both_x, hi_both_x, lo_both_y, hi_both_y = exchange(
        jnp.concatenate([start_field[:1], trans_x[:1]], axis=0),
        jnp.concatenate([start_field[-1:], trans_x[-1:]], axis=0),
        jnp.concatenate([start_field[:, :1], trans_y[:, :1]], axis=1),
        jnp.concatenate([start_field[:, -1:], trans_y[:, -1:]], axis=1),
    )
    lo_x, hi_x, plane_x = lo_both_x[:1], hi_both_x[:1], hi_both_x[1:]
    lo_y, hi_y, plane_y = lo_both_y[:, :1], hi_both_y[:, :1], hi_both_y[:, 1:]

    zero_plane = jnp.zeros_like(trans_z[..., :1])
    tx_lo = trans_x
    tx_hi = jnp.concatenate([trans_x[1:], plane_x], axis=0)
    ty_lo = trans_y
    ty_hi = jnp.concatenate([trans_y[:, 1:], plane_y], axis=1)
    tz_lo = trans_z
    tz_hi = jnp.concatenate([trans_z[..., 1:], zero_plane], axis=-1)
    coef = (tx_lo, tx_hi, ty_lo, ty_hi, tz_lo, tz_hi)
    diagonal = accumulation + tx_lo + tx_hi + ty_lo + ty_hi + tz_lo + tz_hi

    total = neighbour_sum(start_field, (lo_x, hi_x, lo_y, hi_y), coef)
    residual0 = right_side - (diagonal * start_field - total)

    vector = residual0
    basis = [vector]
    for step in range(STEPS):
        total = neighbour_sum(vector, field_halo(vector), coef)
        vector = 2.0 * total / diagonal
        basis.append(vector)
    stats = gram(basis)
    stats = all_sum(stats)
    ortho, upper, scale = finish(stats, basis, cells)
    return (ortho, upper, scale)


def solution(mesh):
    in_specs = (
        P("gx", "gy", None),
        P("gx", "gy", None),
        P("gx", "gy", None),
        P("gx", "gy", None),
        P("gx", "gy", None),
        P("gx", "gy", None),
    )
    out_specs = (P(None, "gx", "gy", None), P(), P())
    return jax.shard_map(local, mesh=mesh, in_specs=in_specs, out_specs=out_specs, check_vma=False)
```

```python
import jax
import jax.numpy as jnp
from jax import lax
from jax.sharding import PartitionSpec as P
from jax.experimental import pallas as pl
from jax.experimental.pallas import tpu as pltpu

STEPS = 4


EPS = 1e-06


def shift_pairs(axis, by):
    peers = lax.axis_size(axis)
    return [(i, i + by) for i in range(peers) if 0 <= i + by < peers]


def swap_pairs(axis, parity):
    peers = lax.axis_size(axis)
    pairs = []
    for i in range(parity, peers - 1, 2):
        pairs += [(i, i + 1), (i + 1, i)]
    return pairs


def axis_exchange(to_low, to_high, axis):
    odd = lax.axis_index(axis) % 2 == 1
    even_swap = lax.ppermute(jnp.where(odd, to_low, to_high), axis, swap_pairs(axis, 0))
    odd_swap = lax.ppermute(jnp.where(odd, to_high, to_low), axis, swap_pairs(axis, 1))
    from_low = jnp.where(odd, even_swap, odd_swap)
    from_high = jnp.where(odd, odd_swap, even_swap)
    return from_low, from_high


def exchange(to_low_x, to_high_x, to_low_y, to_high_y):
    from_low_x, from_high_x = axis_exchange(to_low_x, to_high_x, "gx")
    from_low_y, from_high_y = axis_exchange(to_low_y, to_high_y, "gy")
    return from_low_x, from_high_x, from_low_y, from_high_y


def neighbour_sum(u, halo, coef):
    lo_x, hi_x, lo_y, hi_y = halo
    tx_lo, tx_hi, ty_lo, ty_hi, tz_lo, tz_hi = coef
    zero_plane = jnp.zeros_like(u[..., :1])
    u_xm = jnp.concatenate([lo_x, u[:-1]], axis=0)
    u_xp = jnp.concatenate([u[1:], hi_x], axis=0)
    u_ym = jnp.concatenate([lo_y, u[:, :-1]], axis=1)
    u_yp = jnp.concatenate([u[:, 1:], hi_y], axis=1)
    u_zm = jnp.concatenate([zero_plane, u[..., :-1]], axis=-1)
    u_zp = jnp.concatenate([u[..., 1:], zero_plane], axis=-1)
    total = tx_lo * u_xm + tx_hi * u_xp
    total = total + ty_lo * u_ym + ty_hi * u_yp
    total = total + tz_lo * u_zm + tz_hi * u_zp
    return total


def field_halo(u):
    return exchange(u[:1], u[-1:], u[:, :1], u[:, -1:])


def all_sum(x):
    rounds = []
    for axis in ("gy", "gx"):
        n = lax.axis_size(axis)
        if n & (n - 1):
            rounds.append((axis, None))
            continue
        step = 1
        while step < n:
            rounds.append((axis, step))
            step *= 2
    for k, (axis, step) in enumerate(rounds):
        if step is None:
            x = lax.psum(x, axis)
            continue
        other = lax.ppermute(x, axis, [(i, i ^ step) for i in range(lax.axis_size(axis))])
        if k == len(rounds) - 1:
            return x, other
        x = x + other
    return x, jnp.zeros_like(x)


def gram_kernel(size, *refs):
    basis_refs, out_ref = refs[:size], refs[size]
    tile = out_ref.shape
    pairs = [(a, b) for a in range(size) for b in range(a, size)]
    planes, rows, lanes = basis_refs[0].shape
    chunks = lanes // tile[1]

    def plane(i, accs):
        accs = list(accs)
        for c in range(chunks):
            parts = [r[i, :, c * tile[1] : (c + 1) * tile[1]] for r in basis_refs]
            for n, (a, b) in enumerate(pairs):
                accs[n] = accs[n] + parts[a] * parts[b]
        return tuple(accs)

    zero = jnp.zeros((rows, tile[1]), jnp.float32)
    accs = lax.fori_loop(0, planes, plane, tuple(zero for _ in pairs))
    row_ids = lax.broadcasted_iota(jnp.int32, tile, 0)
    lane_ids = lax.broadcasted_iota(jnp.int32, tile, 1)
    packed = jnp.zeros(tile, jnp.float32)
    for n, (a, b) in enumerate(pairs):
        total = jnp.sum(accs[n])
        hit = (lane_ids == 1 + a * size + b) | (lane_ids == 1 + b * size + a)
        if a == 0 and b == 0:
            hit = hit | (lane_ids == 0)
        packed = jnp.where((row_ids == 0) & hit, total, packed)
    out_ref[...] = packed


def gram(basis):
    size = len(basis)
    vmem = pl.BlockSpec(memory_space=pltpu.VMEM)
    return pl.pallas_call(
        lambda *refs: gram_kernel(size, *refs),
        out_shape=jax.ShapeDtypeStruct((1, 128), jnp.float32),
        in_specs=[vmem] * size,
        out_specs=vmem,
    )(*basis)


def finish_kernel(cells, size, stats_ref, other_ref, *refs):
    basis_refs, (ortho_ref, upper_ref, scale_ref) = refs[:size], refs[size:]
    tile = (8, 128)

    def held(i):
        return jnp.full(tile, stats_ref[0, i], jnp.float32) + jnp.full(tile, other_ref[0, i], jnp.float32)

    per_cell = 1.0 / cells
    scale = jnp.sqrt(held(0) * per_cell + EPS)
    unscale = 1.0 / scale
    weight_g = per_cell * (unscale * unscale)
    gram = [[held(1 + a * size + b) * weight_g for b in range(size)] for a in range(size)]
    upper = [[None] * size for _ in range(size)]
    recip = [None] * size
    for row in range(size):
        value = gram[row][row]
        for prev in range(row):
            value = value - upper[prev][row] * upper[prev][row]
        pivot = jnp.sqrt(value)
        upper[row][row] = pivot
        recip[row] = 1.0 / pivot
        for col in range(row + 1, size):
            value = gram[row][col]
            for prev in range(row):
                value = value - upper[prev][row] * upper[prev][col]
            upper[row][col] = value * recip[row]
    inverse = [[None] * size for _ in range(size)]
    for col in range(size):
        for row in reversed(range(col + 1)):
            if row == col:
                inverse[row][col] = recip[row]
                continue
            value = jnp.zeros(tile, jnp.float32)
            for inner in range(row + 1, col + 1):
                value = value - upper[row][inner] * inverse[inner][col]
            inverse[row][col] = value * recip[row]
    rows = lax.broadcasted_iota(jnp.int32, tile, 0)
    cols = lax.broadcasted_iota(jnp.int32, tile, 1)
    packed = jnp.zeros(tile, jnp.float32)
    for row in range(size):
        for col in range(row, size):
            packed = jnp.where((rows == row) & (cols == col), upper[row][col], packed)
    upper_ref[...] = packed[: upper_ref.shape[0], : upper_ref.shape[1]]
    scale_ref[...] = scale[:1, :1]
    lanes = basis_refs[0].shape[-1] // tile[1]
    weight = [
        [jnp.tile(inverse[j][k] * unscale, (1, lanes)) if j <= k else None for k in range(size)]
        for j in range(size)
    ]

    def plane(i, carry):
        parts = [basis_refs[j][i] for j in range(size)]
        for k in range(size):
            acc = parts[0] * weight[0][k]
            for j in range(1, k + 1):
                acc = acc + parts[j] * weight[j][k]
            ortho_ref[k, i] = acc
        return carry

    lax.fori_loop(0, basis_refs[0].shape[0], plane, 0)


def finish(stats, basis, cells):
    size = len(basis)
    vmem = pl.BlockSpec(memory_space=pltpu.VMEM)
    ortho, upper, scale = pl.pallas_call(
        lambda *refs: finish_kernel(float(cells), size, *refs),
        out_shape=(
            jax.ShapeDtypeStruct((size,) + basis[0].shape, jnp.float32),
            jax.ShapeDtypeStruct((size, size), jnp.float32),
            jax.ShapeDtypeStruct((1, 1), jnp.float32),
        ),
        in_specs=[pl.BlockSpec(memory_space=pltpu.SMEM)] * 2 + [vmem] * size,
        out_specs=(vmem, vmem, vmem),
    )(*stats, *basis)
    return ortho, upper, scale.reshape(())


def local(start_field, right_side, accumulation, trans_x, trans_y, trans_z):
    size_x, size_y, size_z = start_field.shape
    cells = size_x * size_y * size_z * lax.axis_size("gx") * lax.axis_size("gy")

    lo_both_x, hi_both_x, lo_both_y, hi_both_y = exchange(
        jnp.concatenate([start_field[:1], trans_x[:1]], axis=0),
        jnp.concatenate([start_field[-1:], trans_x[-1:]], axis=0),
        jnp.concatenate([start_field[:, :1], trans_y[:, :1]], axis=1),
        jnp.concatenate([start_field[:, -1:], trans_y[:, -1:]], axis=1),
    )
    lo_x, hi_x, plane_x = lo_both_x[:1], hi_both_x[:1], hi_both_x[1:]
    lo_y, hi_y, plane_y = lo_both_y[:, :1], hi_both_y[:, :1], hi_both_y[:, 1:]

    zero_plane = jnp.zeros_like(trans_z[..., :1])
    tx_lo = trans_x
    tx_hi = jnp.concatenate([trans_x[1:], plane_x], axis=0)
    ty_lo = trans_y
    ty_hi = jnp.concatenate([trans_y[:, 1:], plane_y], axis=1)
    tz_lo = trans_z
    tz_hi = jnp.concatenate([trans_z[..., 1:], zero_plane], axis=-1)
    coef = (tx_lo, tx_hi, ty_lo, ty_hi, tz_lo, tz_hi)
    diagonal = accumulation + tx_lo + tx_hi + ty_lo + ty_hi + tz_lo + tz_hi

    total = neighbour_sum(start_field, (lo_x, hi_x, lo_y, hi_y), coef)
    residual0 = right_side - (diagonal * start_field - total)

    vector = residual0
    basis = [vector]
    for step in range(STEPS):
        total = neighbour_sum(vector, field_halo(vector), coef)
        vector = 2.0 * total / diagonal
        basis.append(vector)
    stats = gram(basis)
    stats = all_sum(stats)
    ortho, upper, scale = finish(stats, basis, cells)
    return (ortho, upper, scale)


def solution(mesh):
    in_specs = (
        P("gx", "gy", None),
        P("gx", "gy", None),
        P("gx", "gy", None),
        P("gx", "gy", None),
        P("gx", "gy", None),
        P("gx", "gy", None),
    )
    out_specs = (P(None, "gx", "gy", None), P(), P())
    return jax.shard_map(local, mesh=mesh, in_specs=in_specs, out_specs=out_specs, check_vma=False)
```

```python
import jax
import jax.numpy as jnp
from jax import lax
from jax.sharding import PartitionSpec as P
from jax.experimental import pallas as pl
from jax.experimental.pallas import tpu as pltpu

STEPS = 4


EPS = 1e-06


def shift_pairs(axis, by):
    peers = lax.axis_size(axis)
    return [(i, i + by) for i in range(peers) if 0 <= i + by < peers]


def swap_pairs(axis, parity):
    peers = lax.axis_size(axis)
    pairs = []
    for i in range(parity, peers - 1, 2):
        pairs += [(i, i + 1), (i + 1, i)]
    return pairs


def axis_exchange(to_low, to_high, axis):
    odd = lax.axis_index(axis) % 2 == 1
    even_swap = lax.ppermute(jnp.where(odd, to_low, to_high), axis, swap_pairs(axis, 0))
    odd_swap = lax.ppermute(jnp.where(odd, to_high, to_low), axis, swap_pairs(axis, 1))
    from_low = jnp.where(odd, even_swap, odd_swap)
    from_high = jnp.where(odd, odd_swap, even_swap)
    return from_low, from_high


def exchange(to_low_x, to_high_x, to_low_y, to_high_y):
    from_low_x, from_high_x = axis_exchange(to_low_x, to_high_x, "gx")
    from_low_y, from_high_y = axis_exchange(to_low_y, to_high_y, "gy")
    return from_low_x, from_high_x, from_low_y, from_high_y


def neighbour_sum(u, halo, coef):
    lo_x, hi_x, lo_y, hi_y = halo
    tx_lo, tx_hi, ty_lo, ty_hi, tz_lo, tz_hi = coef
    zero_plane = jnp.zeros_like(u[..., :1])
    u_xm = jnp.concatenate([lo_x, u[:-1]], axis=0)
    u_xp = jnp.concatenate([u[1:], hi_x], axis=0)
    u_ym = jnp.concatenate([lo_y, u[:, :-1]], axis=1)
    u_yp = jnp.concatenate([u[:, 1:], hi_y], axis=1)
    u_zm = jnp.concatenate([zero_plane, u[..., :-1]], axis=-1)
    u_zp = jnp.concatenate([u[..., 1:], zero_plane], axis=-1)
    total = tx_lo * u_xm + tx_hi * u_xp
    total = total + ty_lo * u_ym + ty_hi * u_yp
    total = total + tz_lo * u_zm + tz_hi * u_zp
    return total


def field_halo(u):
    return exchange(u[:1], u[-1:], u[:, :1], u[:, -1:])


def all_sum(x):
    for axis in ("gy", "gx"):
        n = lax.axis_size(axis)
        if n & (n - 1):
            x = lax.psum(x, axis)
            continue
        step = 1
        while step < n:
            x = x + lax.ppermute(x, axis, [(i, i ^ step) for i in range(n)])
            step *= 2
    return x


def gram_kernel(size, *refs):
    basis_refs, out_ref = refs[:size], refs[size]
    tile = out_ref.shape
    pairs = [(a, b) for a in range(size) for b in range(a, size)]
    planes, rows, lanes = basis_refs[0].shape
    chunks = lanes // tile[1]

    def plane(i, accs):
        accs = list(accs)
        for c in range(chunks):
            parts = [r[i, :, c * tile[1] : (c + 1) * tile[1]] for r in basis_refs]
            for n, (a, b) in enumerate(pairs):
                accs[n] = accs[n] + parts[a] * parts[b]
        return tuple(accs)

    zero = jnp.zeros((rows, tile[1]), jnp.float32)
    accs = lax.fori_loop(0, planes, plane, tuple(zero for _ in pairs))
    row_ids = lax.broadcasted_iota(jnp.int32, tile, 0)
    lane_ids = lax.broadcasted_iota(jnp.int32, tile, 1)
    packed = jnp.zeros(tile, jnp.float32)
    for n, (a, b) in enumerate(pairs):
        total = jnp.sum(accs[n])
        hit = (lane_ids == 1 + a * size + b) | (lane_ids == 1 + b * size + a)
        if a == 0 and b == 0:
            hit = hit | (lane_ids == 0)
        packed = jnp.where((row_ids == 0) & hit, total, packed)
    out_ref[...] = packed


def gram(basis):
    size = len(basis)
    vmem = pl.BlockSpec(memory_space=pltpu.VMEM)
    return pl.pallas_call(
        lambda *refs: gram_kernel(size, *refs),
        out_shape=jax.ShapeDtypeStruct((1, 128), jnp.float32),
        in_specs=[vmem] * size,
        out_specs=vmem,
    )(*basis)


def finish_kernel(cells, size, stats_ref, *refs):
    basis_refs, (ortho_ref, upper_ref, scale_ref) = refs[:size], refs[size:]
    tile = (8, 128)

    def held(i):
        return jnp.broadcast_to(stats_ref[:, i : i + 1], tile)

    per_cell = 1.0 / cells
    scale = jnp.sqrt(held(0) * per_cell + EPS)
    unscale = 1.0 / scale
    weight_g = per_cell * (unscale * unscale)
    gram = [[held(1 + a * size + b) * weight_g for b in range(size)] for a in range(size)]
    upper = [[None] * size for _ in range(size)]
    recip = [None] * size
    for row in range(size):
        value = gram[row][row]
        for prev in range(row):
            value = value - upper[prev][row] * upper[prev][row]
        pivot = jnp.sqrt(value)
        upper[row][row] = pivot
        recip[row] = 1.0 / pivot
        for col in range(row + 1, size):
            value = gram[row][col]
            for prev in range(row):
                value = value - upper[prev][row] * upper[prev][col]
            upper[row][col] = value * recip[row]
    inverse = [[None] * size for _ in range(size)]
    for col in range(size):
        for row in reversed(range(col + 1)):
            if row == col:
                inverse[row][col] = recip[row]
                continue
            value = jnp.zeros(tile, jnp.float32)
            for inner in range(row + 1, col + 1):
                value = value - upper[row][inner] * inverse[inner][col]
            inverse[row][col] = value * recip[row]
    rows = lax.broadcasted_iota(jnp.int32, tile, 0)
    cols = lax.broadcasted_iota(jnp.int32, tile, 1)
    packed = jnp.zeros(tile, jnp.float32)
    for row in range(size):
        for col in range(row, size):
            packed = jnp.where((rows == row) & (cols == col), upper[row][col], packed)
    upper_ref[...] = packed[: upper_ref.shape[0], : upper_ref.shape[1]]
    scale_ref[...] = scale[:1, :1]
    lanes = basis_refs[0].shape[-1] // tile[1]
    weight = [
        [jnp.tile(inverse[j][k] * unscale, (1, lanes)) if j <= k else None for k in range(size)]
        for j in range(size)
    ]

    def plane(i, carry):
        parts = [basis_refs[j][i] for j in range(size)]
        for k in range(size):
            acc = parts[0] * weight[0][k]
            for j in range(1, k + 1):
                acc = acc + parts[j] * weight[j][k]
            ortho_ref[k, i] = acc
        return carry

    lax.fori_loop(0, basis_refs[0].shape[0], plane, 0)


def finish(stats, basis, cells):
    size = len(basis)
    vmem = pl.BlockSpec(memory_space=pltpu.VMEM)
    ortho, upper, scale = pl.pallas_call(
        lambda *refs: finish_kernel(float(cells), size, *refs),
        out_shape=(
            jax.ShapeDtypeStruct((size,) + basis[0].shape, jnp.float32),
            jax.ShapeDtypeStruct((size, size), jnp.float32),
            jax.ShapeDtypeStruct((1, 1), jnp.float32),
        ),
        in_specs=[vmem] * (size + 1),
        out_specs=(vmem, vmem, vmem),
    )(stats, *basis)
    return ortho, upper, scale.reshape(())


def local(start_field, right_side, accumulation, trans_x, trans_y, trans_z):
    size_x, size_y, size_z = start_field.shape
    cells = size_x * size_y * size_z * lax.axis_size("gx") * lax.axis_size("gy")

    lo_both_x, hi_both_x, lo_both_y, hi_both_y = exchange(
        jnp.concatenate([start_field[:1], trans_x[:1]], axis=0),
        jnp.concatenate([start_field[-1:], trans_x[-1:]], axis=0),
        jnp.concatenate([start_field[:, :1], trans_y[:, :1]], axis=1),
        jnp.concatenate([start_field[:, -1:], trans_y[:, -1:]], axis=1),
    )
    lo_x, hi_x, plane_x = lo_both_x[:1], hi_both_x[:1], hi_both_x[1:]
    lo_y, hi_y, plane_y = lo_both_y[:, :1], hi_both_y[:, :1], hi_both_y[:, 1:]

    zero_plane = jnp.zeros_like(trans_z[..., :1])
    tx_lo = trans_x
    tx_hi = jnp.concatenate([trans_x[1:], plane_x], axis=0)
    ty_lo = trans_y
    ty_hi = jnp.concatenate([trans_y[:, 1:], plane_y], axis=1)
    tz_lo = trans_z
    tz_hi = jnp.concatenate([trans_z[..., 1:], zero_plane], axis=-1)
    coef = (tx_lo, tx_hi, ty_lo, ty_hi, tz_lo, tz_hi)
    diagonal = accumulation + tx_lo + tx_hi + ty_lo + ty_hi + tz_lo + tz_hi

    total = neighbour_sum(start_field, (lo_x, hi_x, lo_y, hi_y), coef)
    residual0 = right_side - (diagonal * start_field - total)

    vector = residual0
    basis = [vector]
    for step in range(STEPS):
        total = neighbour_sum(vector, field_halo(vector), coef)
        vector = 2.0 * total / diagonal
        basis.append(vector)
    stats = gram(basis)
    stats = all_sum(stats)
    ortho, upper, scale = finish(stats, basis, cells)
    return (ortho, upper, scale)


def solution(mesh):
    in_specs = (
        P("gx", "gy", None),
        P("gx", "gy", None),
        P("gx", "gy", None),
        P("gx", "gy", None),
        P("gx", "gy", None),
        P("gx", "gy", None),
    )
    out_specs = (P(None, "gx", "gy", None), P(), P())
    return jax.shard_map(local, mesh=mesh, in_specs=in_specs, out_specs=out_specs, check_vma=False)
```

```python
import jax
import jax.numpy as jnp
from jax import lax
from jax.sharding import PartitionSpec as P
from jax.experimental import pallas as pl
from jax.experimental.pallas import tpu as pltpu

STEPS = 4


EPS = 1e-06


def shift_pairs(axis, by):
    peers = lax.axis_size(axis)
    return [(i, i + by) for i in range(peers) if 0 <= i + by < peers]


def swap_pairs(axis, parity):
    peers = lax.axis_size(axis)
    pairs = []
    for i in range(parity, peers - 1, 2):
        pairs += [(i, i + 1), (i + 1, i)]
    return pairs


def axis_exchange(to_low, to_high, axis):
    odd = lax.axis_index(axis) % 2 == 1
    even_swap = lax.ppermute(jnp.where(odd, to_low, to_high), axis, swap_pairs(axis, 0))
    odd_swap = lax.ppermute(jnp.where(odd, to_high, to_low), axis, swap_pairs(axis, 1))
    from_low = jnp.where(odd, even_swap, odd_swap)
    from_high = jnp.where(odd, odd_swap, even_swap)
    return from_low, from_high


def exchange(to_low_x, to_high_x, to_low_y, to_high_y):
    from_low_x, from_high_x = axis_exchange(to_low_x, to_high_x, "gx")
    from_low_y, from_high_y = axis_exchange(to_low_y, to_high_y, "gy")
    return from_low_x, from_high_x, from_low_y, from_high_y


def neighbour_sum(u, halo, coef):
    lo_x, hi_x, lo_y, hi_y = halo
    tx_lo, tx_hi, ty_lo, ty_hi, tz_lo, tz_hi = coef
    zero_plane = jnp.zeros_like(u[..., :1])
    u_xm = jnp.concatenate([lo_x, u[:-1]], axis=0)
    u_xp = jnp.concatenate([u[1:], hi_x], axis=0)
    u_ym = jnp.concatenate([lo_y, u[:, :-1]], axis=1)
    u_yp = jnp.concatenate([u[:, 1:], hi_y], axis=1)
    u_zm = jnp.concatenate([zero_plane, u[..., :-1]], axis=-1)
    u_zp = jnp.concatenate([u[..., 1:], zero_plane], axis=-1)
    total = tx_lo * u_xm + tx_hi * u_xp
    total = total + ty_lo * u_ym + ty_hi * u_yp
    total = total + tz_lo * u_zm + tz_hi * u_zp
    return total


def field_halo(u):
    return exchange(u[:1], u[-1:], u[:, :1], u[:, -1:])


def all_sum(x):
    rounds = []
    for axis in ("gy", "gx"):
        n = lax.axis_size(axis)
        if n & (n - 1):
            rounds.append((axis, None))
            continue
        step = 1
        while step < n:
            rounds.append((axis, step))
            step *= 2
    for k, (axis, step) in enumerate(rounds):
        if step is None:
            x = lax.psum(x, axis)
            continue
        other = lax.ppermute(x, axis, [(i, i ^ step) for i in range(lax.axis_size(axis))])
        if k == len(rounds) - 1:
            return x, other
        x = x + other
    return x, jnp.zeros_like(x)


def gram_kernel(size, *refs):
    basis_refs, out_ref = refs[:size], refs[size]
    tile = out_ref.shape
    pairs = [(a, b) for a in range(size) for b in range(a, size)]
    planes, rows, lanes = basis_refs[0].shape
    chunks = lanes // tile[1]

    def plane(i, accs):
        accs = list(accs)
        for c in range(chunks):
            parts = [r[i, :, c * tile[1] : (c + 1) * tile[1]] for r in basis_refs]
            for n, (a, b) in enumerate(pairs):
                accs[n] = accs[n] + parts[a] * parts[b]
        return tuple(accs)

    zero = jnp.zeros((rows, tile[1]), jnp.float32)
    accs = lax.fori_loop(0, planes, plane, tuple(zero for _ in pairs))
    row_ids = lax.broadcasted_iota(jnp.int32, tile, 0)
    lane_ids = lax.broadcasted_iota(jnp.int32, tile, 1)
    packed = jnp.zeros(tile, jnp.float32)
    for n, (a, b) in enumerate(pairs):
        total = jnp.sum(accs[n])
        hit = (lane_ids == 1 + a * size + b) | (lane_ids == 1 + b * size + a)
        if a == 0 and b == 0:
            hit = hit | (lane_ids == 0)
        packed = jnp.where((row_ids == 0) & hit, total, packed)
    out_ref[...] = packed


def gram(basis):
    size = len(basis)
    vmem = pl.BlockSpec(memory_space=pltpu.VMEM)
    return pl.pallas_call(
        lambda *refs: gram_kernel(size, *refs),
        out_shape=jax.ShapeDtypeStruct((1, 128), jnp.float32),
        in_specs=[vmem] * size,
        out_specs=vmem,
    )(*basis)


def finish_kernel(cells, size, stats_ref, other_ref, *refs):
    basis_refs, (ortho_ref, upper_ref, scale_ref) = refs[:size], refs[size:]
    tile = (8, 128)

    def held(i):
        return jnp.broadcast_to(stats_ref[:, i : i + 1] + other_ref[:, i : i + 1], tile)

    per_cell = 1.0 / cells
    scale = jnp.sqrt(held(0) * per_cell + EPS)
    unscale = 1.0 / scale
    weight_g = per_cell * (unscale * unscale)
    gram = [[held(1 + a * size + b) * weight_g for b in range(size)] for a in range(size)]
    upper = [[None] * size for _ in range(size)]
    recip = [None] * size
    for row in range(size):
        value = gram[row][row]
        for prev in range(row):
            value = value - upper[prev][row] * upper[prev][row]
        pivot = jnp.sqrt(value)
        upper[row][row] = pivot
        recip[row] = 1.0 / pivot
        for col in range(row + 1, size):
            value = gram[row][col]
            for prev in range(row):
                value = value - upper[prev][row] * upper[prev][col]
            upper[row][col] = value * recip[row]
    inverse = [[None] * size for _ in range(size)]
    for col in range(size):
        for row in reversed(range(col + 1)):
            if row == col:
                inverse[row][col] = recip[row]
                continue
            value = jnp.zeros(tile, jnp.float32)
            for inner in range(row + 1, col + 1):
                value = value - upper[row][inner] * inverse[inner][col]
            inverse[row][col] = value * recip[row]
    rows = lax.broadcasted_iota(jnp.int32, tile, 0)
    cols = lax.broadcasted_iota(jnp.int32, tile, 1)
    packed = jnp.zeros(tile, jnp.float32)
    for row in range(size):
        for col in range(row, size):
            packed = jnp.where((rows == row) & (cols == col), upper[row][col], packed)
    upper_ref[...] = packed[: upper_ref.shape[0], : upper_ref.shape[1]]
    scale_ref[...] = scale[:1, :1]
    lanes = basis_refs[0].shape[-1] // tile[1]
    weight = [
        [jnp.tile(inverse[j][k] * unscale, (1, lanes)) if j <= k else None for k in range(size)]
        for j in range(size)
    ]

    def plane(i, carry):
        parts = [basis_refs[j][i] for j in range(size)]
        for k in range(size):
            acc = parts[0] * weight[0][k]
            for j in range(1, k + 1):
                acc = acc + parts[j] * weight[j][k]
            ortho_ref[k, i] = acc
        return carry

    lax.fori_loop(0, basis_refs[0].shape[0], plane, 0)


def finish(stats, basis, cells):
    size = len(basis)
    vmem = pl.BlockSpec(memory_space=pltpu.VMEM)
    ortho, upper, scale = pl.pallas_call(
        lambda *refs: finish_kernel(float(cells), size, *refs),
        out_shape=(
            jax.ShapeDtypeStruct((size,) + basis[0].shape, jnp.float32),
            jax.ShapeDtypeStruct((size, size), jnp.float32),
            jax.ShapeDtypeStruct((1, 1), jnp.float32),
        ),
        in_specs=[vmem] * (size + 2),
        out_specs=(vmem, vmem, vmem),
    )(*stats, *basis)
    return ortho, upper, scale.reshape(())


def local(start_field, right_side, accumulation, trans_x, trans_y, trans_z):
    size_x, size_y, size_z = start_field.shape
    cells = size_x * size_y * size_z * lax.axis_size("gx") * lax.axis_size("gy")

    lo_both_x, hi_both_x, lo_both_y, hi_both_y = exchange(
        jnp.concatenate([start_field[:1], trans_x[:1]], axis=0),
        jnp.concatenate([start_field[-1:], trans_x[-1:]], axis=0),
        jnp.concatenate([start_field[:, :1], trans_y[:, :1]], axis=1),
        jnp.concatenate([start_field[:, -1:], trans_y[:, -1:]], axis=1),
    )
    lo_x, hi_x, plane_x = lo_both_x[:1], hi_both_x[:1], hi_both_x[1:]
    lo_y, hi_y, plane_y = lo_both_y[:, :1], hi_both_y[:, :1], hi_both_y[:, 1:]

    zero_plane = jnp.zeros_like(trans_z[..., :1])
    tx_lo = trans_x
    tx_hi = jnp.concatenate([trans_x[1:], plane_x], axis=0)
    ty_lo = trans_y
    ty_hi = jnp.concatenate([trans_y[:, 1:], plane_y], axis=1)
    tz_lo = trans_z
    tz_hi = jnp.concatenate([trans_z[..., 1:], zero_plane], axis=-1)
    coef = (tx_lo, tx_hi, ty_lo, ty_hi, tz_lo, tz_hi)
    diagonal = accumulation + tx_lo + tx_hi + ty_lo + ty_hi + tz_lo + tz_hi

    total = neighbour_sum(start_field, (lo_x, hi_x, lo_y, hi_y), coef)
    residual0 = right_side - (diagonal * start_field - total)

    vector = residual0
    basis = [vector]
    for step in range(STEPS):
        total = neighbour_sum(vector, field_halo(vector), coef)
        vector = 2.0 * total / diagonal
        basis.append(vector)
    stats = gram(basis)
    stats = all_sum(stats)
    ortho, upper, scale = finish(stats, basis, cells)
    return (ortho, upper, scale)


def solution(mesh):
    in_specs = (
        P("gx", "gy", None),
        P("gx", "gy", None),
        P("gx", "gy", None),
        P("gx", "gy", None),
        P("gx", "gy", None),
        P("gx", "gy", None),
    )
    out_specs = (P(None, "gx", "gy", None), P(), P())
    return jax.shard_map(local, mesh=mesh, in_specs=in_specs, out_specs=out_specs, check_vma=False)
```

```python
import jax
import jax.numpy as jnp
from jax import lax
from jax.sharding import PartitionSpec as P
from jax.experimental import pallas as pl
from jax.experimental.pallas import tpu as pltpu

STEPS = 4


EPS = 1e-06


def shift_pairs(axis, by):
    peers = lax.axis_size(axis)
    return [(i, i + by) for i in range(peers) if 0 <= i + by < peers]


def swap_pairs(axis, parity):
    peers = lax.axis_size(axis)
    pairs = []
    for i in range(parity, peers - 1, 2):
        pairs += [(i, i + 1), (i + 1, i)]
    return pairs


def axis_exchange(to_low, to_high, axis):
    odd = lax.axis_index(axis) % 2 == 1
    even_swap = lax.ppermute(jnp.where(odd, to_low, to_high), axis, swap_pairs(axis, 0))
    odd_swap = lax.ppermute(jnp.where(odd, to_high, to_low), axis, swap_pairs(axis, 1))
    from_low = jnp.where(odd, even_swap, odd_swap)
    from_high = jnp.where(odd, odd_swap, even_swap)
    return from_low, from_high


def exchange(to_low_x, to_high_x, to_low_y, to_high_y):
    from_low_x, from_high_x = axis_exchange(to_low_x, to_high_x, "gx")
    from_low_y, from_high_y = axis_exchange(to_low_y, to_high_y, "gy")
    return from_low_x, from_high_x, from_low_y, from_high_y


def neighbour_sum(u, halo, coef):
    lo_x, hi_x, lo_y, hi_y = halo
    tx_lo, tx_hi, ty_lo, ty_hi, tz_lo, tz_hi = coef
    zero_plane = jnp.zeros_like(u[..., :1])
    u_xm = jnp.concatenate([lo_x, u[:-1]], axis=0)
    u_xp = jnp.concatenate([u[1:], hi_x], axis=0)
    u_ym = jnp.concatenate([lo_y, u[:, :-1]], axis=1)
    u_yp = jnp.concatenate([u[:, 1:], hi_y], axis=1)
    u_zm = jnp.concatenate([zero_plane, u[..., :-1]], axis=-1)
    u_zp = jnp.concatenate([u[..., 1:], zero_plane], axis=-1)
    total = tx_lo * u_xm + tx_hi * u_xp
    total = total + ty_lo * u_ym + ty_hi * u_yp
    total = total + tz_lo * u_zm + tz_hi * u_zp
    return total


def face_exchange(u, axis, dim):
    last = u.shape[dim] - 1
    odd = lax.axis_index(axis) % 2 == 1
    to_even = lax.dynamic_slice_in_dim(u, jnp.where(odd, 0, last), 1, axis=dim)
    to_odd = lax.dynamic_slice_in_dim(u, jnp.where(odd, last, 0), 1, axis=dim)
    even_swap = lax.ppermute(to_even, axis, swap_pairs(axis, 0))
    odd_swap = lax.ppermute(to_odd, axis, swap_pairs(axis, 1))
    return jnp.where(odd, even_swap, odd_swap), jnp.where(odd, odd_swap, even_swap)


def field_halo(u):
    return face_exchange(u, "gx", 0) + face_exchange(u, "gy", 1)


def all_sum(x):
    for axis in ("gy", "gx"):
        n = lax.axis_size(axis)
        if n & (n - 1):
            x = lax.psum(x, axis)
            continue
        step = 1
        while step < n:
            x = x + lax.ppermute(x, axis, [(i, i ^ step) for i in range(n)])
            step *= 2
    return x


def gram_kernel(size, *refs):
    basis_refs, out_ref = refs[:size], refs[size]
    tile = out_ref.shape
    pairs = [(a, b) for a in range(size) for b in range(a, size)]
    planes, rows, lanes = basis_refs[0].shape
    chunks = lanes // tile[1]

    def plane(i, accs):
        accs = list(accs)
        for c in range(chunks):
            parts = [r[i, :, c * tile[1] : (c + 1) * tile[1]] for r in basis_refs]
            for n, (a, b) in enumerate(pairs):
                accs[n] = accs[n] + parts[a] * parts[b]
        return tuple(accs)

    zero = jnp.zeros((rows, tile[1]), jnp.float32)
    accs = lax.fori_loop(0, planes, plane, tuple(zero for _ in pairs))
    row_ids = lax.broadcasted_iota(jnp.int32, tile, 0)
    lane_ids = lax.broadcasted_iota(jnp.int32, tile, 1)
    packed = jnp.zeros(tile, jnp.float32)
    for n, (a, b) in enumerate(pairs):
        total = jnp.sum(accs[n])
        hit = (lane_ids == 1 + a * size + b) | (lane_ids == 1 + b * size + a)
        if a == 0 and b == 0:
            hit = hit | (lane_ids == 0)
        packed = jnp.where((row_ids == 0) & hit, total, packed)
    out_ref[...] = packed


def gram(basis):
    size = len(basis)
    vmem = pl.BlockSpec(memory_space=pltpu.VMEM)
    return pl.pallas_call(
        lambda *refs: gram_kernel(size, *refs),
        out_shape=jax.ShapeDtypeStruct((1, 128), jnp.float32),
        in_specs=[vmem] * size,
        out_specs=vmem,
    )(*basis)


def finish_kernel(cells, size, stats_ref, *refs):
    basis_refs, (ortho_ref, upper_ref, scale_ref) = refs[:size], refs[size:]
    tile = (8, 128)

    def held(i):
        return jnp.full(tile, stats_ref[0, i], jnp.float32)

    per_cell = 1.0 / cells
    scale = jnp.sqrt(held(0) * per_cell + EPS)
    unscale = 1.0 / scale
    weight_g = per_cell * (unscale * unscale)
    gram = [[held(1 + a * size + b) * weight_g for b in range(size)] for a in range(size)]
    upper = [[None] * size for _ in range(size)]
    recip = [None] * size
    for row in range(size):
        value = gram[row][row]
        for prev in range(row):
            value = value - upper[prev][row] * upper[prev][row]
        pivot = jnp.sqrt(value)
        upper[row][row] = pivot
        recip[row] = 1.0 / pivot
        for col in range(row + 1, size):
            value = gram[row][col]
            for prev in range(row):
                value = value - upper[prev][row] * upper[prev][col]
            upper[row][col] = value * recip[row]
    inverse = [[None] * size for _ in range(size)]
    for col in range(size):
        for row in reversed(range(col + 1)):
            if row == col:
                inverse[row][col] = recip[row]
                continue
            value = jnp.zeros(tile, jnp.float32)
            for inner in range(row + 1, col + 1):
                value = value - upper[row][inner] * inverse[inner][col]
            inverse[row][col] = value * recip[row]
    rows = lax.broadcasted_iota(jnp.int32, tile, 0)
    cols = lax.broadcasted_iota(jnp.int32, tile, 1)
    packed = jnp.zeros(tile, jnp.float32)
    for row in range(size):
        for col in range(row, size):
            packed = jnp.where((rows == row) & (cols == col), upper[row][col], packed)
    upper_ref[...] = packed[: upper_ref.shape[0], : upper_ref.shape[1]]
    scale_ref[...] = scale[:1, :1]
    lanes = basis_refs[0].shape[-1] // tile[1]
    weight = [
        [jnp.tile(inverse[j][k] * unscale, (1, lanes)) if j <= k else None for k in range(size)]
        for j in range(size)
    ]

    def plane(i, carry):
        parts = [basis_refs[j][i] for j in range(size)]
        for k in range(size):
            acc = parts[0] * weight[0][k]
            for j in range(1, k + 1):
                acc = acc + parts[j] * weight[j][k]
            ortho_ref[k, i] = acc
        return carry

    lax.fori_loop(0, basis_refs[0].shape[0], plane, 0)


def finish(stats, basis, cells):
    size = len(basis)
    vmem = pl.BlockSpec(memory_space=pltpu.VMEM)
    ortho, upper, scale = pl.pallas_call(
        lambda *refs: finish_kernel(float(cells), size, *refs),
        out_shape=(
            jax.ShapeDtypeStruct((size,) + basis[0].shape, jnp.float32),
            jax.ShapeDtypeStruct((size, size), jnp.float32),
            jax.ShapeDtypeStruct((1, 1), jnp.float32),
        ),
        in_specs=[pl.BlockSpec(memory_space=pltpu.SMEM)] + [vmem] * size,
        out_specs=(vmem, vmem, vmem),
    )(stats, *basis)
    return ortho, upper, scale.reshape(())


def local(start_field, right_side, accumulation, trans_x, trans_y, trans_z):
    size_x, size_y, size_z = start_field.shape
    cells = size_x * size_y * size_z * lax.axis_size("gx") * lax.axis_size("gy")

    lo_both_x, hi_both_x, lo_both_y, hi_both_y = exchange(
        jnp.concatenate([start_field[:1], trans_x[:1]], axis=0),
        jnp.concatenate([start_field[-1:], trans_x[-1:]], axis=0),
        jnp.concatenate([start_field[:, :1], trans_y[:, :1]], axis=1),
        jnp.concatenate([start_field[:, -1:], trans_y[:, -1:]], axis=1),
    )
    lo_x, hi_x, plane_x = lo_both_x[:1], hi_both_x[:1], hi_both_x[1:]
    lo_y, hi_y, plane_y = lo_both_y[:, :1], hi_both_y[:, :1], hi_both_y[:, 1:]

    zero_plane = jnp.zeros_like(trans_z[..., :1])
    tx_lo = trans_x
    tx_hi = jnp.concatenate([trans_x[1:], plane_x], axis=0)
    ty_lo = trans_y
    ty_hi = jnp.concatenate([trans_y[:, 1:], plane_y], axis=1)
    tz_lo = trans_z
    tz_hi = jnp.concatenate([trans_z[..., 1:], zero_plane], axis=-1)
    coef = (tx_lo, tx_hi, ty_lo, ty_hi, tz_lo, tz_hi)
    diagonal = accumulation + tx_lo + tx_hi + ty_lo + ty_hi + tz_lo + tz_hi

    total = neighbour_sum(start_field, (lo_x, hi_x, lo_y, hi_y), coef)
    residual0 = right_side - (diagonal * start_field - total)

    vector = residual0
    basis = [vector]
    for step in range(STEPS):
        total = neighbour_sum(vector, field_halo(vector), coef)
        vector = 2.0 * total / diagonal
        basis.append(vector)
    stats = gram(basis)
    stats = all_sum(stats)
    ortho, upper, scale = finish(stats, basis, cells)
    return (ortho, upper, scale)


def solution(mesh):
    in_specs = (
        P("gx", "gy", None),
        P("gx", "gy", None),
        P("gx", "gy", None),
        P("gx", "gy", None),
        P("gx", "gy", None),
        P("gx", "gy", None),
    )
    out_specs = (P(None, "gx", "gy", None), P(), P())
    return jax.shard_map(local, mesh=mesh, in_specs=in_specs, out_specs=out_specs, check_vma=False)
```
